512 devices in a mesh: lat: 32 (over z_lo, x), lon: 16 (over y, z_hi, core).
Axes of the slice: x: 4, y: 4, z: 16 (z_hi: 2, z_lo: 8; z = z_hi * 8 + z_lo), core: 2. Of those that a mesh axis runs over, the one named last changes fastest.
Arguments:
- cotangent: bfloat16 [512, 1440, 256], P('lat', 'lon'), may hold values from -6 to 6
- legendre: bfloat16 [512, 384, 192], P('lat', 'lon'), may hold values from -0.25 to 0.25
- spectral_weight: bfloat16 [256, 256], replicated, may hold values from -0.375 to 0.375
- skip_weight: bfloat16 [256, 256], replicated, may hold values from -0.375 to 0.375
Outputs:
- grad_input: bfloat16 [512, 1440, 256], P('lat', 'lon')
The draws below stay inside these ranges and needn't reach their ends.
All inputs are finite; a program needn't handle non-finite values.
Results may differ from the reference program's by a relative error of at most 0.015.
Values may be sent and summed in bfloat16 or wider, within the bound.
No kernel may reach another device: no remote copies, remote signals or barrier semaphores. Data moves between devices by JAX's collectives and lax.ppermute only.
A program may use at most 64 MiB of HBM per device.

```python
import math
import jax
import jax.numpy as jnp
from jax import lax

C = 256
NLON = 1440
MM = 384
LH = 192
LAT_DEV = 16
NLAT = 512


def block_levels(own_key, extent, split, least, largest):
    loudness = 1.0
    for position, blocks in split:
        draws = jax.random.uniform(jax.random.fold_in(jax.random.fold_in(own_key, 6), position), (blocks,), jnp.float32, least / len(split), largest / len(split))
        loudness = loudness * jnp.repeat(jnp.exp(draws), extent[position] // blocks).reshape((-1,) + (1,) * (len(extent) - 1 - position))
    return loudness


def scatter_about(rng, dims, scale, bound, shards=(), kind=jnp.bfloat16):
    drawn = scale * jax.random.normal(rng, dims, jnp.float32)
    if shards:
        drawn = drawn * block_levels(rng, dims, shards, -0.22, 0.18)
    return jnp.clip(drawn, -bound, bound).astype(kind)


def setup_inputs(seed: int = 0) -> dict:
    key_of = jax.random.split(jax.random.key(seed), 5)
    return {
        "cotangent": scatter_about(key_of[0], (NLAT, NLON, C), 1.0, 6.0, ((0, 32), (1, 16))),
        "legendre": scatter_about(key_of[1], (NLAT, MM, LH), NLAT ** -0.5, 0.25, ((0, 32), (1, 16))),
        "spectral_weight": scatter_about(key_of[2], (C, C), C ** -0.5, 0.375),
        "skip_weight": scatter_about(key_of[3], (C, C), C ** -0.5, 0.375),
    }


def degree_masks(wave_start, wave_count, half_deg):
    wavenum = wave_start + lax.broadcasted_iota(jnp.int32, (wave_count, half_deg), 0)
    degree = 2 * lax.broadcasted_iota(jnp.int32, (wave_count, half_deg), 1)
    parity = wavenum % 2
    return (degree + parity >= wavenum, degree + 1 - parity >= wavenum)

def mix_channels(spectral, spectral_weight):
    width = spectral.shape[-1]
    flat_values = spectral.reshape(-1, width)
    mixed_out = jnp.dot(flat_values, spectral_weight.T, preferred_element_type=jnp.float32)
    return mixed_out.astype(jnp.bfloat16).reshape(spectral.shape)

def band_total(basis, values):
    band_count = basis.shape[0] // LAT_DEV
    basis_bands = basis.reshape((band_count, LAT_DEV) + basis.shape[1:])
    value_bands = values.reshape((band_count, LAT_DEV) + values.shape[1:])

    def advance(running, operands):
        contrib = jnp.einsum('rmk,rmpc->kmpc', operands[0].astype(jnp.float32), operands[1].astype(jnp.float32))
        contrib = lax.optimization_barrier(contrib.astype(jnp.bfloat16)).astype(jnp.float32)
        return (running + contrib, None)
    initial = jnp.zeros((basis.shape[2], basis.shape[1], 2, values.shape[-1]), jnp.float32)
    running, unused = lax.scan(advance, initial, (basis_bands, value_bands))
    return running

def reference(cotangent, legendre, spectral_weight, skip_weight):
    count_lat, count_lon, width = cotangent.shape
    count_wave = legendre.shape[1]
    half_deg = legendre.shape[2]
    half_rows = count_lat // 2
    norm_scale = math.sqrt(2.0 / count_lon)
    spectrum = jnp.fft.rfft(cotangent.astype(jnp.float32), axis=1)[:, :count_wave]
    coeffs = (norm_scale * jnp.stack([jnp.real(spectrum), jnp.imag(spectrum)], axis=2)).astype(jnp.bfloat16)
    mask_even, mask_odd = degree_masks(0, count_wave, half_deg)
    north_rows = legendre[:half_rows]
    south_rows = legendre[half_rows:]
    north_basis = jnp.where(mask_even[None], north_rows, jnp.zeros_like(north_rows))
    south_basis = jnp.where(mask_odd[None], south_rows, jnp.zeros_like(south_rows))
    north_wide = coeffs[:half_rows].astype(jnp.float32)
    south_wide = coeffs[half_rows:].astype(jnp.float32)
    comb_even = (north_wide + south_wide).astype(jnp.bfloat16)
    comb_odd = (north_wide - south_wide).astype(jnp.bfloat16)
    degree_split = jnp.stack([band_total(north_basis, comb_even), band_total(south_basis, comb_odd)]).astype(jnp.bfloat16)
    mixed_out = mix_channels(degree_split, spectral_weight)
    proj_even = jnp.einsum('rmk,kmpc->rmpc', north_basis.astype(jnp.float32), mixed_out[0].astype(jnp.float32))
    proj_even = lax.optimization_barrier(proj_even.astype(jnp.bfloat16)).astype(jnp.float32)
    proj_odd = jnp.einsum('rmk,kmpc->rmpc', south_basis.astype(jnp.float32), mixed_out[1].astype(jnp.float32))
    proj_odd = lax.optimization_barrier(proj_odd.astype(jnp.bfloat16)).astype(jnp.float32)
    grad_coeffs = jnp.concatenate([proj_even + proj_odd, proj_even - proj_odd], 0).astype(jnp.bfloat16)
    real_part = grad_coeffs[:, :, 0, :].astype(jnp.float32)
    imag_part = grad_coeffs[:, :, 1, :].astype(jnp.float32)
    padding = count_lon // 2 + 1 - count_wave
    spectral_full = lax.complex(jnp.pad(real_part, ((0, 0), (0, padding), (0, 0))), jnp.pad(imag_part, ((0, 0), (0, padding), (0, 0))))
    grid_part = norm_scale * (0.5 * count_lon * jnp.fft.irfft(spectral_full, n=count_lon, axis=1) + 0.5 * real_part[:, 0:1, :])
    grid_part = grid_part.astype(jnp.bfloat16)
    skip_term = jnp.dot(cotangent.reshape(-1, width), skip_weight.T, preferred_element_type=jnp.float32).reshape(cotangent.shape)
    return (grid_part.astype(jnp.float32) + skip_term).astype(jnp.bfloat16)
```

```python
import math

import numpy as np

import jax
import jax.numpy as jnp
from jax import lax
from jax.sharding import PartitionSpec as P


def fourier_table(count_lon, count_wave):
    longitude = lax.broadcasted_iota(jnp.int32, (count_lon, count_wave), 0)
    wavenum = lax.broadcasted_iota(jnp.int32, (count_lon, count_wave), 1)
    phases = longitude * wavenum % count_lon
    angles = phases.astype(jnp.float32) * (2.0 * math.pi / count_lon)
    norm_scale = math.sqrt(2.0 / count_lon)
    stacked = jnp.stack([norm_scale * jnp.cos(angles), -norm_scale * jnp.sin(angles)], axis=2)
    return stacked.reshape(count_lon, 2 * count_wave)


def unit_slots(lat_count, units_per_dev):
    first = [(units_per_dev * t) // 4 for t in range(lat_count)]
    last = [(units_per_dev * t + units_per_dev - 1) // 4 for t in range(lat_count)]
    return np.stack([np.array(first), np.array(last)], axis=1)


def shards(cotangent, legendre, spectral_weight, skip_weight):
    lat_rows, lon_dev, width = cotangent.shape
    lat_count = lax.axis_size("lat")
    lon_count = lax.axis_size("lon")
    count_lon = lon_dev * lon_count
    wave_dev = legendre.shape[1]
    half_deg = legendre.shape[2]
    all_rows = lat_rows * lat_count
    half_rows = all_rows // 2
    fourier = fourier_table(count_lon, wave_dev * lon_count)

    spectra = jnp.einsum(
        "rlc,lk->rkc",
        lax.all_to_all(cotangent, "lon", split_axis=0, concat_axis=1, tiled=True).astype(
            jnp.float32
        ),
        fourier,
        precision=lax.Precision.HIGHEST,
    )
    coeffs = lax.all_to_all(
        spectra.astype(jnp.bfloat16), "lon", split_axis=1, concat_axis=0, tiled=True
    )
    units_total = wave_dev * 4
    units_per_dev = units_total // lat_count
    unit_width = width // 2
    units = coeffs.reshape(lat_rows, units_total, unit_width)
    gathered = lax.all_to_all(
        units.reshape(lat_rows, lat_count, units_per_dev, unit_width),
        "lat",
        split_axis=1,
        concat_axis=0,
        tiled=True,
    ).reshape(all_rows, units_per_dev, unit_width)

    slots = unit_slots(lat_count, units_per_dev)
    basis_send = jnp.take(legendre, jnp.asarray(slots.reshape(-1)), axis=1)
    basis_recv = lax.all_to_all(
        basis_send.reshape(lat_rows, lat_count, 2, half_deg),
        "lat",
        split_axis=1,
        concat_axis=0,
        tiled=True,
    ).reshape(all_rows, 2, half_deg)

    band = lax.axis_index("lat")
    unit_ids = units_per_dev * band + jnp.arange(units_per_dev)
    local_wave = unit_ids // 4
    use_last = (local_wave - (units_per_dev * band) // 4) > 0
    basis = jnp.where(
        use_last[None, :, None], basis_recv[:, 1:2, :], basis_recv[:, 0:1, :]
    )
    wavenum = lax.axis_index("lon") * wave_dev + local_wave
    degree = 2 * jnp.arange(half_deg)
    parity = wavenum % 2
    mask_even = degree[None, :] + parity[:, None] >= wavenum[:, None]
    mask_odd = degree[None, :] + 1 - parity[:, None] >= wavenum[:, None]
    north_basis = jnp.where(mask_even[None], basis[:half_rows], jnp.zeros_like(basis[:half_rows]))
    south_basis = jnp.where(mask_odd[None], basis[half_rows:], jnp.zeros_like(basis[half_rows:]))

    north_wide = gathered[:half_rows].astype(jnp.float32)
    south_wide = gathered[half_rows:].astype(jnp.float32)
    comb_even = (north_wide + south_wide).astype(jnp.bfloat16)
    comb_odd = (north_wide - south_wide).astype(jnp.bfloat16)
    deg_even = jnp.einsum(
        "nuk,nuc->ukc", north_basis, comb_even, preferred_element_type=jnp.float32
    ).astype(jnp.bfloat16)
    deg_odd = jnp.einsum(
        "nuk,nuc->ukc", south_basis, comb_odd, preferred_element_type=jnp.float32
    ).astype(jnp.bfloat16)
    proj_even = jnp.einsum(
        "nuk,ukc->nuc", north_basis, deg_even, preferred_element_type=jnp.float32
    ).astype(jnp.bfloat16).astype(jnp.float32)
    proj_odd = jnp.einsum(
        "nuk,ukc->nuc", south_basis, deg_odd, preferred_element_type=jnp.float32
    ).astype(jnp.bfloat16).astype(jnp.float32)
    grad_units = jnp.concatenate([proj_even + proj_odd, proj_even - proj_odd], 0).astype(
        jnp.bfloat16
    )
    returned = lax.all_to_all(
        grad_units.reshape(lat_count, lat_rows, units_per_dev, unit_width),
        "lat",
        split_axis=0,
        concat_axis=2,
        tiled=True,
    ).reshape(lat_rows, 2 * wave_dev, width)

    grid_part = jnp.einsum(
        "rkc,lk->rlc",
        lax.all_to_all(returned, "lon", split_axis=0, concat_axis=1, tiled=True).astype(
            jnp.float32
        ),
        fourier,
        precision=lax.Precision.HIGHEST,
    )
    spatial = lax.all_to_all(
        grid_part.astype(jnp.bfloat16), "lon", split_axis=1, concat_axis=0, tiled=True
    )
    stacked_in = jnp.concatenate([spatial, cotangent], axis=-1).reshape(-1, 2 * width)
    stacked_w = jnp.concatenate([spectral_weight, skip_weight], axis=1)
    out = jnp.dot(stacked_in, stacked_w.T, preferred_element_type=jnp.float32)
    return out.astype(jnp.bfloat16).reshape(cotangent.shape)


def solution(mesh):
    return jax.shard_map(
        shards,
        mesh=mesh,
        in_specs=(P("lat", "lon", None), P("lat", "lon", None), P(), P()),
        out_specs=P("lat", "lon", None),
        check_vma=False,
    )
```

```python
import math

import numpy as np

import jax
import jax.numpy as jnp
from jax import lax
from jax.sharding import PartitionSpec as P


def fourier_table(count_lon, count_wave):
    longitude = lax.broadcasted_iota(jnp.int32, (count_lon, 2 * count_wave), 0)
    column = lax.broadcasted_iota(jnp.int32, (count_lon, 2 * count_wave), 1)
    phases = (longitude * (column // 2) + (count_lon // 4) * (column % 2)) % count_lon
    angles = phases.astype(jnp.float32) * (2.0 * math.pi / count_lon)
    table = math.sqrt(2.0 / count_lon) * jnp.cos(angles)
    high = lax.reduce_precision(table, exponent_bits=8, mantissa_bits=7)
    return high.astype(jnp.bfloat16), (table - high).astype(jnp.bfloat16)


def split_dot(table_hi, table_lo, values, dims):
    dot = lambda t: lax.dot_general(t, values, dims, preferred_element_type=jnp.float32)
    return dot(table_hi) + dot(table_lo)


def unit_slots(lat_count, units_per_dev):
    first = [(units_per_dev * t) // 4 for t in range(lat_count)]
    last = [(units_per_dev * t + units_per_dev - 1) // 4 for t in range(lat_count)]
    return np.stack([np.array(first), np.array(last)], axis=1)


def shards(cotangent, legendre, spectral_weight, skip_weight):
    lat_rows, lon_dev, width = cotangent.shape
    lat_count = lax.axis_size("lat")
    lon_count = lax.axis_size("lon")
    count_lon = lon_dev * lon_count
    wave_dev = legendre.shape[1]
    half_deg = legendre.shape[2]
    all_rows = lat_rows * lat_count
    half_rows = all_rows // 2
    table_hi, table_lo = fourier_table(count_lon, wave_dev * lon_count)

    row_grid = lax.all_to_all(cotangent, "lon", 0, 0, tiled=True).reshape(count_lon, width)
    spectra = split_dot(table_hi, table_lo, row_grid, (((0,), (0,)), ((), ())))
    coeffs = lax.all_to_all(
        spectra.astype(jnp.bfloat16).reshape(lon_count, 2 * wave_dev, width), "lon", 0, 0, tiled=True
    )
    units_total = wave_dev * 4
    units_per_dev = units_total // lat_count
    unit_width = width // 2
    unit_send = coeffs.reshape(lat_rows, lat_count, units_per_dev * unit_width)
    slots = unit_slots(lat_count, units_per_dev)
    basis_send = jnp.take(legendre, jnp.asarray(slots.reshape(-1)), axis=1).reshape(
        lat_rows, lat_count, 2 * half_deg
    )
    payload = jnp.concatenate([unit_send, basis_send], axis=-1).transpose(1, 0, 2)
    arrived = lax.all_to_all(payload, "lat", 0, 0, tiled=True).reshape(all_rows, -1)
    gathered = arrived[:, : units_per_dev * unit_width].reshape(all_rows, units_per_dev, unit_width)
    basis_recv = arrived[:, units_per_dev * unit_width :].reshape(all_rows, 2, half_deg)

    band = lax.axis_index("lat")
    unit_ids = units_per_dev * band + jnp.arange(units_per_dev)
    local_wave = unit_ids // 4
    use_last = (local_wave - (units_per_dev * band) // 4) > 0
    basis = jnp.where(
        use_last[None, :, None], basis_recv[:, 1:2, :], basis_recv[:, 0:1, :]
    )
    wavenum = lax.axis_index("lon") * wave_dev + local_wave
    degree = 2 * jnp.arange(half_deg)
    parity = wavenum % 2
    mask_even = degree[None, :] + parity[:, None] >= wavenum[:, None]
    mask_odd = degree[None, :] + 1 - parity[:, None] >= wavenum[:, None]
    north_basis = jnp.where(mask_even[None], basis[:half_rows], jnp.zeros_like(basis[:half_rows]))
    south_basis = jnp.where(mask_odd[None], basis[half_rows:], jnp.zeros_like(basis[half_rows:]))

    north_wide = gathered[:half_rows].astype(jnp.float32)
    south_wide = gathered[half_rows:].astype(jnp.float32)
    comb_even = (north_wide + south_wide).astype(jnp.bfloat16)
    comb_odd = (north_wide - south_wide).astype(jnp.bfloat16)
    deg_even = jnp.einsum(
        "nuk,nuc->ukc", north_basis, comb_even, preferred_element_type=jnp.float32
    ).astype(jnp.bfloat16)
    deg_odd = jnp.einsum(
        "nuk,nuc->ukc", south_basis, comb_odd, preferred_element_type=jnp.float32
    ).astype(jnp.bfloat16)
    proj_even = jnp.einsum(
        "nuk,ukc->nuc", north_basis, deg_even, preferred_element_type=jnp.float32
    ).astype(jnp.bfloat16).astype(jnp.float32)
    proj_odd = jnp.einsum(
        "nuk,ukc->nuc", south_basis, deg_odd, preferred_element_type=jnp.float32
    ).astype(jnp.bfloat16).astype(jnp.float32)
    grad_units = jnp.concatenate([proj_even + proj_odd, proj_even - proj_odd], 0).astype(
        jnp.bfloat16
    )
    returned = lax.all_to_all(
        grad_units.reshape(lat_count, lat_rows, units_per_dev * unit_width), "lat", 0, 0, tiled=True
    ).transpose(1, 0, 2).reshape(lat_rows, 2 * wave_dev, width)

    row_coeffs = lax.all_to_all(returned, "lon", 0, 0, tiled=True).reshape(2 * wave_dev * lon_count, width)
    grid_part = split_dot(table_hi, table_lo, row_coeffs, (((1,), (0,)), ((), ())))
    spatial = lax.all_to_all(
        grid_part.astype(jnp.bfloat16).reshape(lon_count, lon_dev, width), "lon", 0, 0, tiled=True
    )
    stacked_in = jnp.concatenate([spatial, cotangent], axis=-1).reshape(-1, 2 * width)
    stacked_w = jnp.concatenate([spectral_weight, skip_weight], axis=1)
    out = jnp.dot(stacked_in, stacked_w.T, preferred_element_type=jnp.float32)
    return out.astype(jnp.bfloat16).reshape(cotangent.shape)


def solution(mesh):
    return jax.shard_map(
        shards,
        mesh=mesh,
        in_specs=(P("lat", "lon", None), P("lat", "lon", None), P(), P()),
        out_specs=P("lat", "lon", None),
        check_vma=False,
    )
```

```python
import math

import numpy as np

import jax
import jax.numpy as jnp
from jax import lax
from jax.sharding import PartitionSpec as P


def fourier_table(count_lon, count_wave):
    longitude = lax.broadcasted_iota(jnp.int32, (count_lon, 2 * count_wave), 0)
    column = lax.broadcasted_iota(jnp.int32, (count_lon, 2 * count_wave), 1)
    phases = (longitude * (column // 2) + (count_lon // 4) * (column % 2)) % count_lon
    angles = phases.astype(jnp.float32) * (2.0 * math.pi / count_lon)
    table = math.sqrt(2.0 / count_lon) * jnp.cos(angles)
    high = lax.reduce_precision(table, exponent_bits=8, mantissa_bits=7)
    return lax.optimization_barrier((high.astype(jnp.bfloat16), (table - high).astype(jnp.bfloat16)))


def split_dot(table_hi, table_lo, values, dims):
    dot = lambda t: lax.dot_general(t, values, dims, preferred_element_type=jnp.float32)
    return dot(table_hi) + dot(table_lo)


def unit_slots(lat_count, units_per_dev):
    first = [(units_per_dev * t) // 4 for t in range(lat_count)]
    last = [(units_per_dev * t + units_per_dev - 1) // 4 for t in range(lat_count)]
    return np.stack([np.array(first), np.array(last)], axis=1)


def shards(cotangent, legendre, spectral_weight, skip_weight):
    lat_rows, lon_dev, width = cotangent.shape
    lat_count = lax.axis_size("lat")
    lon_count = lax.axis_size("lon")
    count_lon = lon_dev * lon_count
    wave_dev = legendre.shape[1]
    half_deg = legendre.shape[2]
    all_rows = lat_rows * lat_count
    half_rows = all_rows // 2
    table_hi, table_lo = fourier_table(count_lon, wave_dev * lon_count)

    row_grid = lax.all_to_all(cotangent, "lon", 0, 0, tiled=True).reshape(count_lon, width)
    spectra = split_dot(table_hi, table_lo, row_grid, (((0,), (0,)), ((), ())))
    coeffs = lax.all_to_all(
        spectra.astype(jnp.bfloat16).reshape(lon_count, 2 * wave_dev, width), "lon", 0, 0, tiled=True
    )
    units_total = wave_dev * 4
    units_per_dev = units_total // lat_count
    unit_width = width // 2
    unit_send = coeffs.reshape(lat_rows, lat_count, units_per_dev * unit_width)
    slots = unit_slots(lat_count, units_per_dev)
    basis_send = jnp.take(legendre, jnp.asarray(slots.reshape(-1)), axis=1).reshape(
        lat_rows, lat_count, 2 * half_deg
    )
    payload = jnp.concatenate([unit_send, basis_send], axis=-1).transpose(1, 0, 2)
    arrived = lax.all_to_all(payload, "lat", 0, 0, tiled=True).reshape(all_rows, -1)
    gathered = arrived[:, : units_per_dev * unit_width].reshape(all_rows, units_per_dev, unit_width)
    basis_recv = arrived[:, units_per_dev * unit_width :].reshape(all_rows, 2, half_deg)

    band = lax.axis_index("lat")
    unit_ids = units_per_dev * band + jnp.arange(units_per_dev)
    local_wave = unit_ids // 4
    use_last = (local_wave - (units_per_dev * band) // 4) > 0
    basis = jnp.where(
        use_last[None, :, None], basis_recv[:, 1:2, :], basis_recv[:, 0:1, :]
    )
    wavenum = lax.axis_index("lon") * wave_dev + local_wave
    degree = 2 * jnp.arange(half_deg)
    parity = wavenum % 2
    mask_even = degree[None, :] + parity[:, None] >= wavenum[:, None]
    mask_odd = degree[None, :] + 1 - parity[:, None] >= wavenum[:, None]
    north_basis = jnp.where(mask_even[None], basis[:half_rows], jnp.zeros_like(basis[:half_rows]))
    south_basis = jnp.where(mask_odd[None], basis[half_rows:], jnp.zeros_like(basis[half_rows:]))

    north_wide = gathered[:half_rows].astype(jnp.float32)
    south_wide = gathered[half_rows:].astype(jnp.float32)
    comb_even = (north_wide + south_wide).astype(jnp.bfloat16)
    comb_odd = (north_wide - south_wide).astype(jnp.bfloat16)
    deg_even = jnp.einsum(
        "nuk,nuc->ukc", north_basis, comb_even, preferred_element_type=jnp.float32
    ).astype(jnp.bfloat16)
    deg_odd = jnp.einsum(
        "nuk,nuc->ukc", south_basis, comb_odd, preferred_element_type=jnp.float32
    ).astype(jnp.bfloat16)
    proj_even = jnp.einsum(
        "nuk,ukc->nuc", north_basis, deg_even, preferred_element_type=jnp.float32
    ).astype(jnp.bfloat16).astype(jnp.float32)
    proj_odd = jnp.einsum(
        "nuk,ukc->nuc", south_basis, deg_odd, preferred_element_type=jnp.float32
    ).astype(jnp.bfloat16).astype(jnp.float32)
    grad_units = jnp.concatenate([proj_even + proj_odd, proj_even - proj_odd], 0).astype(
        jnp.bfloat16
    )
    returned = lax.all_to_all(
        grad_units.reshape(lat_count, lat_rows, units_per_dev * unit_width), "lat", 0, 0, tiled=True
    ).transpose(1, 0, 2).reshape(lat_rows, 2 * wave_dev, width)

    row_coeffs = lax.all_to_all(returned, "lon", 0, 0, tiled=True).reshape(2 * wave_dev * lon_count, width)
    grid_part = split_dot(table_hi, table_lo, row_coeffs, (((1,), (0,)), ((), ())))
    spatial = lax.all_to_all(
        grid_part.astype(jnp.bfloat16).reshape(lon_count, lon_dev, width), "lon", 0, 0, tiled=True
    )
    stacked_in = jnp.concatenate([spatial, cotangent], axis=-1).reshape(-1, 2 * width)
    stacked_w = jnp.concatenate([spectral_weight, skip_weight], axis=1)
    out = jnp.dot(stacked_in, stacked_w.T, preferred_element_type=jnp.float32)
    return out.astype(jnp.bfloat16).reshape(cotangent.shape)


def solution(mesh):
    return jax.shard_map(
        shards,
        mesh=mesh,
        in_specs=(P("lat", "lon", None), P("lat", "lon", None), P(), P()),
        out_specs=P("lat", "lon", None),
        check_vma=False,
    )
```

```python
import math

import numpy as np

import jax
import jax.numpy as jnp
from jax import lax
from jax.sharding import PartitionSpec as P


def fourier_table(count_lon, count_wave):
    longitude = lax.broadcasted_iota(jnp.int32, (count_lon, 2 * count_wave), 0)
    column = lax.broadcasted_iota(jnp.int32, (count_lon, 2 * count_wave), 1)
    phases = (longitude * (column // 2) + (count_lon // 4) * (column % 2)) % count_lon
    angles = phases.astype(jnp.float32) * (2.0 * math.pi / count_lon)
    table = math.sqrt(2.0 / count_lon) * jnp.cos(angles)
    high = lax.reduce_precision(table, exponent_bits=8, mantissa_bits=7)
    return lax.optimization_barrier((high.astype(jnp.bfloat16), (table - high).astype(jnp.bfloat16)))


def split_dot(table_hi, table_lo, values, dims):
    dot = lambda t: lax.dot_general(t, values, dims, preferred_element_type=jnp.float32)
    return dot(table_hi) + dot(table_lo)


def unit_slots(lat_count, units_per_dev):
    first = [(units_per_dev * t) // 4 for t in range(lat_count)]
    last = [(units_per_dev * t + units_per_dev - 1) // 4 for t in range(lat_count)]
    return np.stack([np.array(first), np.array(last)], axis=1)


def shards(cotangent, legendre, spectral_weight, skip_weight):
    lat_rows, lon_dev, width = cotangent.shape
    lat_count = lax.axis_size("lat")
    lon_count = lax.axis_size("lon")
    count_lon = lon_dev * lon_count
    wave_dev = legendre.shape[1]
    half_deg = legendre.shape[2]
    all_rows = lat_rows * lat_count
    half_rows = all_rows // 2
    table_hi, table_lo = fourier_table(count_lon, wave_dev * lon_count)
    skip_term = jnp.einsum("rlc,dc->rld", cotangent, skip_weight, preferred_element_type=jnp.float32)

    row_grid = lax.all_to_all(cotangent, "lon", 0, 0, tiled=True).reshape(count_lon, width)
    spectra = split_dot(table_hi, table_lo, row_grid, (((0,), (0,)), ((), ())))
    coeffs = lax.all_to_all(
        spectra.astype(jnp.bfloat16).reshape(lon_count, 2 * wave_dev, width), "lon", 0, 0, tiled=True
    )
    units_total = wave_dev * 4
    units_per_dev = units_total // lat_count
    unit_width = width // 2
    unit_send = coeffs.reshape(lat_rows, lat_count, units_per_dev * unit_width).transpose(1, 0, 2)
    slots = unit_slots(lat_count, units_per_dev)
    basis_send = jnp.stack(
        [jnp.concatenate([legendre[:, a], legendre[:, b]], axis=-1) for a, b in slots.tolist()]
    )
    payload = jnp.concatenate([unit_send, basis_send], axis=-1)
    arrived = lax.all_to_all(payload, "lat", 0, 0, tiled=True).reshape(all_rows, -1)
    gathered = arrived[:, : units_per_dev * unit_width].reshape(all_rows, units_per_dev, unit_width)
    basis_recv = arrived[:, units_per_dev * unit_width :].reshape(all_rows, 2, half_deg)

    band = lax.axis_index("lat")
    unit_ids = units_per_dev * band + jnp.arange(units_per_dev)
    local_wave = unit_ids // 4
    use_last = (local_wave - (units_per_dev * band) // 4) > 0
    basis = jnp.where(
        use_last[None, :, None], basis_recv[:, 1:2, :], basis_recv[:, 0:1, :]
    )
    wavenum = lax.axis_index("lon") * wave_dev + local_wave
    degree = 2 * jnp.arange(half_deg)
    parity = wavenum % 2
    mask_even = degree[None, :] + parity[:, None] >= wavenum[:, None]
    mask_odd = degree[None, :] + 1 - parity[:, None] >= wavenum[:, None]
    north_basis = jnp.where(mask_even[None], basis[:half_rows], jnp.zeros_like(basis[:half_rows]))
    south_basis = jnp.where(mask_odd[None], basis[half_rows:], jnp.zeros_like(basis[half_rows:]))

    north_wide = gathered[:half_rows].astype(jnp.float32)
    south_wide = gathered[half_rows:].astype(jnp.float32)
    comb_even = (north_wide + south_wide).astype(jnp.bfloat16)
    comb_odd = (north_wide - south_wide).astype(jnp.bfloat16)
    deg_even = jnp.einsum(
        "nuk,nuc->ukc", north_basis, comb_even, preferred_element_type=jnp.float32
    ).astype(jnp.bfloat16)
    deg_odd = jnp.einsum(
        "nuk,nuc->ukc", south_basis, comb_odd, preferred_element_type=jnp.float32
    ).astype(jnp.bfloat16)
    proj_even = jnp.einsum(
        "nuk,ukc->nuc", north_basis, deg_even, preferred_element_type=jnp.float32
    ).astype(jnp.bfloat16).astype(jnp.float32)
    proj_odd = jnp.einsum(
        "nuk,ukc->nuc", south_basis, deg_odd, preferred_element_type=jnp.float32
    ).astype(jnp.bfloat16).astype(jnp.float32)
    grad_units = jnp.concatenate([proj_even + proj_odd, proj_even - proj_odd], 0).astype(
        jnp.bfloat16
    )
    returned = lax.all_to_all(
        grad_units.reshape(lat_count, lat_rows, units_per_dev * unit_width), "lat", 0, 0, tiled=True
    ).transpose(1, 0, 2).reshape(lat_rows, 2 * wave_dev, width)

    row_coeffs = lax.all_to_all(returned, "lon", 0, 0, tiled=True).reshape(2 * wave_dev * lon_count, width)
    grid_part = split_dot(table_hi, table_lo, row_coeffs, (((1,), (0,)), ((), ())))
    spatial = lax.all_to_all(
        grid_part.astype(jnp.bfloat16).reshape(lon_count, lon_dev, width), "lon", 0, 0, tiled=True
    )
    mixed = jnp.einsum("rlc,dc->rld", spatial, spectral_weight, preferred_element_type=jnp.float32)
    return (mixed + skip_term).astype(jnp.bfloat16)


def solution(mesh):
    return jax.shard_map(
        shards,
        mesh=mesh,
        in_specs=(P("lat", "lon", None), P("lat", "lon", None), P(), P()),
        out_specs=P("lat", "lon", None),
        check_vma=False,
    )
```

```python
import math

import numpy as np

import jax
import jax.numpy as jnp
from jax import lax
from jax.sharding import PartitionSpec as P


def fourier_table(count_lon, count_wave):
    longitude = lax.broadcasted_iota(jnp.int32, (count_lon, 2 * count_wave), 0)
    column = lax.broadcasted_iota(jnp.int32, (count_lon, 2 * count_wave), 1)
    phases = (longitude * (column // 2) + (count_lon // 4) * (column % 2)) % count_lon
    angles = phases.astype(jnp.float32) * (2.0 * math.pi / count_lon)
    table = math.sqrt(2.0 / count_lon) * jnp.cos(angles)
    high = lax.reduce_precision(table, exponent_bits=8, mantissa_bits=7)
    return lax.optimization_barrier((high.astype(jnp.bfloat16), (table - high).astype(jnp.bfloat16)))


def split_dot(table_hi, table_lo, values, dims):
    dot = lambda t: lax.dot_general(t, values, dims, preferred_element_type=jnp.float32)
    return dot(table_hi) + dot(table_lo)


def unit_slots(lat_count, units_per_dev):
    first = [(units_per_dev * t) // 4 for t in range(lat_count)]
    last = [(units_per_dev * t + units_per_dev - 1) // 4 for t in range(lat_count)]
    return np.stack([np.array(first), np.array(last)], axis=1)


def shards(cotangent, legendre, spectral_weight, skip_weight):
    lat_rows, lon_dev, width = cotangent.shape
    lat_count = lax.axis_size("lat")
    lon_count = lax.axis_size("lon")
    count_lon = lon_dev * lon_count
    wave_dev = legendre.shape[1]
    half_deg = legendre.shape[2]
    all_rows = lat_rows * lat_count
    half_rows = all_rows // 2
    table_hi, table_lo = fourier_table(count_lon, wave_dev * lon_count)
    skip_term = jnp.einsum("rlc,dc->rld", cotangent, skip_weight, preferred_element_type=jnp.float32)

    row_grid = lax.all_to_all(cotangent, "lon", 0, 0, tiled=True).reshape(count_lon, width)
    spectra = split_dot(table_hi, table_lo, row_grid, (((0,), (0,)), ((), ())))
    coeffs = lax.all_to_all(
        spectra.astype(jnp.bfloat16).reshape(lon_count, 2 * wave_dev, width), "lon", 0, 0, tiled=True
    )
    units_total = wave_dev * 4
    units_per_dev = units_total // lat_count
    unit_width = width // 2
    unit_send = coeffs.reshape(lat_rows, lat_count, units_per_dev * unit_width).transpose(1, 0, 2)
    slots = unit_slots(lat_count, units_per_dev)
    basis_send = jnp.stack(
        [jnp.concatenate([legendre[:, a], legendre[:, b]], axis=-1) for a, b in slots.tolist()]
    )
    payload = jnp.concatenate([unit_send, basis_send], axis=-1)
    arrived = lax.all_to_all(payload, "lat", 0, 0, tiled=True).reshape(all_rows, -1)
    gathered = arrived[:, : units_per_dev * unit_width].reshape(all_rows, units_per_dev, unit_width)
    basis_recv = arrived[:, units_per_dev * unit_width :].reshape(all_rows, 2, half_deg)

    band = lax.axis_index("lat")
    unit_ids = units_per_dev * band + jnp.arange(units_per_dev)
    local_wave = unit_ids // 4
    use_last = (local_wave - (units_per_dev * band) // 4) > 0
    basis = jnp.where(
        use_last[None, :, None], basis_recv[:, 1:2, :], basis_recv[:, 0:1, :]
    )
    wavenum = lax.axis_index("lon") * wave_dev + local_wave
    degree = 2 * jnp.arange(half_deg)
    parity = wavenum % 2
    mask_even = degree[None, :] + parity[:, None] >= wavenum[:, None]
    mask_odd = degree[None, :] + 1 - parity[:, None] >= wavenum[:, None]
    north_basis = jnp.where(mask_even[None], basis[:half_rows], jnp.zeros_like(basis[:half_rows]))
    south_basis = jnp.where(mask_odd[None], basis[half_rows:], jnp.zeros_like(basis[half_rows:]))

    north_wide = gathered[:half_rows].astype(jnp.float32)
    south_wide = gathered[half_rows:].astype(jnp.float32)
    comb_even = (north_wide + south_wide).astype(jnp.bfloat16)
    comb_odd = (north_wide - south_wide).astype(jnp.bfloat16)
    deg_even = jnp.einsum(
        "nuk,nuc->ukc", north_basis, comb_even, preferred_element_type=jnp.float32
    ).astype(jnp.bfloat16)
    deg_odd = jnp.einsum(
        "nuk,nuc->ukc", south_basis, comb_odd, preferred_element_type=jnp.float32
    ).astype(jnp.bfloat16)
    proj_even = jnp.einsum(
        "nuk,ukc->nuc", north_basis, deg_even, preferred_element_type=jnp.float32
    ).astype(jnp.bfloat16).astype(jnp.float32)
    proj_odd = jnp.einsum(
        "nuk,ukc->nuc", south_basis, deg_odd, preferred_element_type=jnp.float32
    ).astype(jnp.bfloat16).astype(jnp.float32)
    grad_units = jnp.concatenate([proj_even + proj_odd, proj_even - proj_odd], 0).astype(
        jnp.bfloat16
    )
    returned = lax.all_to_all(
        grad_units.reshape(lat_count, lat_rows, units_per_dev * unit_width), "lat", 0, 0, tiled=True
    ).transpose(1, 0, 2).reshape(lat_rows, 2 * wave_dev, width)

    halves = 2
    group = lon_count // halves
    pair_rows = lat_rows // group
    own_half = (lax.axis_index("lon") // 2) % halves
    by_pair = returned.reshape(lon_count // 4, 1, 2, pair_rows, 2 * wave_dev, width)
    pair_send = jnp.broadcast_to(
        by_pair, (lon_count // 4, halves, 2, pair_rows, 2 * wave_dev, width)
    ).reshape(lon_count, pair_rows, 2 * wave_dev, width)
    pair_coeffs = lax.all_to_all(pair_send, "lon", 0, 0, tiled=True)
    pair_coeffs = pair_coeffs.transpose(1, 0, 2, 3).reshape(pair_rows, 2 * wave_dev * lon_count, width)
    half_table = lambda t: lax.dynamic_index_in_dim(
        t.reshape(lon_count // 4, halves, 2, lon_dev, -1), own_half, axis=1, keepdims=False
    ).reshape(group * lon_dev, -1)
    half_grid = split_dot(
        half_table(table_hi), half_table(table_lo), pair_coeffs, (((1,), (1,)), ((), ()))
    )
    half_send = half_grid.astype(jnp.bfloat16).reshape(group, lon_dev, pair_rows, width).transpose(0, 2, 1, 3)
    lon_ids = np.arange(lon_count).reshape(lon_count // 4, halves, 2)
    half_groups = [lon_ids[:, h, :].reshape(-1).tolist() for h in range(halves)]
    spatial = lax.all_to_all(
        half_send, "lon", 0, 0, tiled=True, axis_index_groups=half_groups
    ).reshape(lat_rows, lon_dev, width)
    mixed = jnp.einsum("rlc,dc->rld", spatial, spectral_weight, preferred_element_type=jnp.float32)
    return (mixed + skip_term).astype(jnp.bfloat16)


def solution(mesh):
    return jax.shard_map(
        shards,
        mesh=mesh,
        in_specs=(P("lat", "lon", None), P("lat", "lon", None), P(), P()),
        out_specs=P("lat", "lon", None),
        check_vma=False,
    )
```

```python
import math

import numpy as np

import jax
import jax.numpy as jnp
from jax import lax
from jax.sharding import PartitionSpec as P


def fourier_table(longitude, count_lon, count_wave):
    column = lax.broadcasted_iota(jnp.int32, (longitude.shape[0], 2 * count_wave), 1)
    phases = (longitude[:, None] * (column // 2) + (count_lon // 4) * (column % 2)) % count_lon
    angles = phases.astype(jnp.float32) * (2.0 * math.pi / count_lon)
    table = math.sqrt(2.0 / count_lon) * jnp.cos(angles)
    high = lax.reduce_precision(table, exponent_bits=8, mantissa_bits=7)
    return lax.optimization_barrier((high.astype(jnp.bfloat16), (table - high).astype(jnp.bfloat16)))


def split_dot(table_hi, table_lo, values, dims):
    dot = lambda t: lax.dot_general(t, values, dims, preferred_element_type=jnp.float32)
    return dot(table_hi) + dot(table_lo)


def unit_slots(lat_count, units_per_dev):
    first = [(units_per_dev * t) // 4 for t in range(lat_count)]
    last = [(units_per_dev * t + units_per_dev - 1) // 4 for t in range(lat_count)]
    return np.stack([np.array(first), np.array(last)], axis=1)


def shards(cotangent, legendre, spectral_weight, skip_weight):
    lat_rows, lon_dev, width = cotangent.shape
    lat_count = lax.axis_size("lat")
    lon_count = lax.axis_size("lon")
    count_lon = lon_dev * lon_count
    wave_dev = legendre.shape[1]
    half_deg = legendre.shape[2]
    all_rows = lat_rows * lat_count
    half_rows = all_rows // 2
    skip_term = jnp.einsum("rlc,dc->rld", cotangent, skip_weight, preferred_element_type=jnp.float32)

    halves = 2
    group = lon_count // halves
    pair_rows = lat_rows // group
    own_half = (lax.axis_index("lon") // 2) % halves
    position = jnp.arange(group * lon_dev) // lon_dev
    longitude = lon_dev * ((position // 2) * 4 + 2 * own_half + position % 2) + jnp.arange(
        group * lon_dev
    ) % lon_dev
    table_hi, table_lo = fourier_table(longitude, count_lon, wave_dev * lon_count)
    lon_ids = np.arange(lon_count).reshape(lon_count // 4, halves, 2)
    half_groups = [lon_ids[:, h, :].reshape(-1).tolist() for h in range(halves)]

    pair_grid = lax.all_to_all(
        cotangent.reshape(group, pair_rows, lon_dev, width), "lon", 0, 0, tiled=True,
        axis_index_groups=half_groups,
    ).transpose(1, 0, 2, 3).reshape(pair_rows, group * lon_dev, width)
    partial = split_dot(table_hi, table_lo, pair_grid, (((0,), (1,)), ((), ())))
    partial_recv = lax.all_to_all(
        partial.astype(jnp.bfloat16).reshape(lon_count, 2 * wave_dev, pair_rows, width), "lon", 0, 0, tiled=True
    ).reshape(lon_count // 4, halves, 2, 2 * wave_dev, pair_rows, width)
    coeffs = jnp.sum(partial_recv.astype(jnp.float32), axis=1).astype(jnp.bfloat16)
    coeffs = coeffs.transpose(0, 1, 3, 2, 4).reshape(lat_rows, 2 * wave_dev, width)
    units_total = wave_dev * 4
    units_per_dev = units_total // lat_count
    unit_width = width // 2
    unit_send = coeffs.reshape(lat_rows, lat_count, units_per_dev * unit_width).transpose(1, 0, 2)
    slots = unit_slots(lat_count, units_per_dev)
    basis_send = jnp.stack(
        [jnp.concatenate([legendre[:, a], legendre[:, b]], axis=-1) for a, b in slots.tolist()]
    )
    payload = jnp.concatenate([unit_send, basis_send], axis=-1)
    arrived = lax.all_to_all(payload, "lat", 0, 0, tiled=True).reshape(all_rows, -1)
    gathered = arrived[:, : units_per_dev * unit_width].reshape(all_rows, units_per_dev, unit_width)
    basis_recv = arrived[:, units_per_dev * unit_width :].reshape(all_rows, 2, half_deg)

    band = lax.axis_index("lat")
    unit_ids = units_per_dev * band + jnp.arange(units_per_dev)
    local_wave = unit_ids // 4
    use_last = (local_wave - (units_per_dev * band) // 4) > 0
    basis = jnp.where(
        use_last[None, :, None], basis_recv[:, 1:2, :], basis_recv[:, 0:1, :]
    )
    wavenum = lax.axis_index("lon") * wave_dev + local_wave
    degree = 2 * jnp.arange(half_deg)
    parity = wavenum % 2
    mask_even = degree[None, :] + parity[:, None] >= wavenum[:, None]
    mask_odd = degree[None, :] + 1 - parity[:, None] >= wavenum[:, None]
    north_basis = jnp.where(mask_even[None], basis[:half_rows], jnp.zeros_like(basis[:half_rows]))
    south_basis = jnp.where(mask_odd[None], basis[half_rows:], jnp.zeros_like(basis[half_rows:]))

    north_wide = gathered[:half_rows].astype(jnp.float32)
    south_wide = gathered[half_rows:].astype(jnp.float32)
    comb_even = (north_wide + south_wide).astype(jnp.bfloat16)
    comb_odd = (north_wide - south_wide).astype(jnp.bfloat16)
    deg_even = jnp.einsum(
        "nuk,nuc->ukc", north_basis, comb_even, preferred_element_type=jnp.float32
    ).astype(jnp.bfloat16)
    deg_odd = jnp.einsum(
        "nuk,nuc->ukc", south_basis, comb_odd, preferred_element_type=jnp.float32
    ).astype(jnp.bfloat16)
    proj_even = jnp.einsum(
        "nuk,ukc->nuc", north_basis, deg_even, preferred_element_type=jnp.float32
    ).astype(jnp.bfloat16).astype(jnp.float32)
    proj_odd = jnp.einsum(
        "nuk,ukc->nuc", south_basis, deg_odd, preferred_element_type=jnp.float32
    ).astype(jnp.bfloat16).astype(jnp.float32)
    grad_units = jnp.concatenate([proj_even + proj_odd, proj_even - proj_odd], 0).astype(
        jnp.bfloat16
    )
    returned = lax.all_to_all(
        grad_units.reshape(lat_count, lat_rows, units_per_dev * unit_width), "lat", 0, 0, tiled=True
    ).transpose(1, 0, 2).reshape(lat_rows, 2 * wave_dev, width)

    by_pair = returned.reshape(lon_count // 4, 1, 2, pair_rows, 2 * wave_dev, width)
    pair_send = jnp.broadcast_to(
        by_pair, (lon_count // 4, halves, 2, pair_rows, 2 * wave_dev, width)
    ).reshape(lon_count, pair_rows, 2 * wave_dev, width)
    pair_coeffs = lax.all_to_all(pair_send, "lon", 0, 0, tiled=True)
    pair_coeffs = pair_coeffs.transpose(1, 0, 2, 3).reshape(pair_rows, 2 * wave_dev * lon_count, width)
    half_grid = split_dot(table_hi, table_lo, pair_coeffs, (((1,), (1,)), ((), ())))
    half_send = half_grid.astype(jnp.bfloat16).reshape(group, lon_dev, pair_rows, width).transpose(0, 2, 1, 3)
    spatial = lax.all_to_all(
        half_send, "lon", 0, 0, tiled=True, axis_index_groups=half_groups
    ).reshape(lat_rows, lon_dev, width)
    mixed = jnp.einsum("rlc,dc->rld", spatial, spectral_weight, preferred_element_type=jnp.float32)
    return (mixed + skip_term).astype(jnp.bfloat16)


def solution(mesh):
    return jax.shard_map(
        shards,
        mesh=mesh,
        in_specs=(P("lat", "lon", None), P("lat", "lon", None), P(), P()),
        out_specs=P("lat", "lon", None),
        check_vma=False,
    )
```

```python
import math

import numpy as np

import jax
import jax.numpy as jnp
from jax import lax
from jax.sharding import PartitionSpec as P


def fourier_table(longitude, count_lon, count_wave):
    column = lax.broadcasted_iota(jnp.int32, (longitude.shape[0], 2 * count_wave), 1)
    phases = (longitude[:, None] * (column // 2) + (count_lon // 4) * (column % 2)) % count_lon
    angles = phases.astype(jnp.float32) * (2.0 * math.pi / count_lon)
    table = math.sqrt(2.0 / count_lon) * jnp.cos(angles)
    high = lax.reduce_precision(table, exponent_bits=8, mantissa_bits=7)
    return lax.optimization_barrier((high.astype(jnp.bfloat16), (table - high).astype(jnp.bfloat16)))


def split_dot(table_hi, table_lo, values, dims):
    dot = lambda t: lax.dot_general(t, values, dims, preferred_element_type=jnp.float32)
    return dot(table_hi) + dot(table_lo)


def unit_slots(lat_count, units_per_dev):
    first = [(units_per_dev * t) // 4 for t in range(lat_count)]
    last = [(units_per_dev * t + units_per_dev - 1) // 4 for t in range(lat_count)]
    return np.stack([np.array(first), np.array(last)], axis=1)


def shards(cotangent, legendre, spectral_weight, skip_weight):
    lat_rows, lon_dev, width = cotangent.shape
    lat_count = lax.axis_size("lat")
    lon_count = lax.axis_size("lon")
    count_lon = lon_dev * lon_count
    wave_dev = legendre.shape[1]
    half_deg = legendre.shape[2]
    all_rows = lat_rows * lat_count
    half_rows = all_rows // 2
    units_total = wave_dev * 4
    units_per_dev = units_total // lat_count
    slots = unit_slots(lat_count, units_per_dev)
    basis_send = jnp.stack(
        [jnp.concatenate([legendre[:, a], legendre[:, b]], axis=-1) for a, b in slots.tolist()]
    )
    basis_recv = lax.all_to_all(basis_send, "lat", 0, 0, tiled=True).reshape(all_rows, 2, half_deg)
    basis_recv, cotangent_held = lax.optimization_barrier((basis_recv, cotangent))
    skip_term = jnp.einsum("rlc,dc->rld", cotangent, skip_weight, preferred_element_type=jnp.float32)

    halves = 2
    group = lon_count // halves
    pair_rows = lat_rows // group
    own_half = (lax.axis_index("lon") // 2) % halves
    position = jnp.arange(group * lon_dev) // lon_dev
    longitude = lon_dev * ((position // 2) * 4 + 2 * own_half + position % 2) + jnp.arange(
        group * lon_dev
    ) % lon_dev
    table_hi, table_lo = fourier_table(longitude, count_lon, wave_dev * lon_count)
    lon_ids = np.arange(lon_count).reshape(lon_count // 4, halves, 2)
    half_groups = [lon_ids[:, h, :].reshape(-1).tolist() for h in range(halves)]

    pair_grid = lax.all_to_all(
        cotangent_held.reshape(group, pair_rows, lon_dev, width), "lon", 0, 0, tiled=True,
        axis_index_groups=half_groups,
    ).transpose(1, 0, 2, 3).reshape(pair_rows, group * lon_dev, width)
    partial = split_dot(table_hi, table_lo, pair_grid, (((0,), (1,)), ((), ())))
    partial_recv = lax.all_to_all(
        partial.astype(jnp.bfloat16).reshape(lon_count, 2 * wave_dev, pair_rows, width), "lon", 0, 0, tiled=True
    ).reshape(lon_count // 4, halves, 2, 2 * wave_dev, pair_rows, width)
    coeffs = jnp.sum(partial_recv.astype(jnp.float32), axis=1).astype(jnp.bfloat16)
    coeffs = coeffs.transpose(0, 1, 3, 2, 4).reshape(lat_rows, 2 * wave_dev, width)
    unit_width = width // 2
    unit_send = coeffs.reshape(lat_rows, lat_count, units_per_dev * unit_width).transpose(1, 0, 2)
    arrived = lax.all_to_all(unit_send, "lat", 0, 0, tiled=True).reshape(all_rows, -1)
    gathered = arrived.reshape(all_rows, units_per_dev, unit_width)

    band = lax.axis_index("lat")
    unit_ids = units_per_dev * band + jnp.arange(units_per_dev)
    local_wave = unit_ids // 4
    use_last = (local_wave - (units_per_dev * band) // 4) > 0
    basis = jnp.where(
        use_last[None, :, None], basis_recv[:, 1:2, :], basis_recv[:, 0:1, :]
    )
    wavenum = lax.axis_index("lon") * wave_dev + local_wave
    degree = 2 * jnp.arange(half_deg)
    parity = wavenum % 2
    mask_even = degree[None, :] + parity[:, None] >= wavenum[:, None]
    mask_odd = degree[None, :] + 1 - parity[:, None] >= wavenum[:, None]
    north_basis = jnp.where(mask_even[None], basis[:half_rows], jnp.zeros_like(basis[:half_rows]))
    south_basis = jnp.where(mask_odd[None], basis[half_rows:], jnp.zeros_like(basis[half_rows:]))

    north_wide = gathered[:half_rows].astype(jnp.float32)
    south_wide = gathered[half_rows:].astype(jnp.float32)
    comb_even = (north_wide + south_wide).astype(jnp.bfloat16)
    comb_odd = (north_wide - south_wide).astype(jnp.bfloat16)
    deg_even = jnp.einsum(
        "nuk,nuc->ukc", north_basis, comb_even, preferred_element_type=jnp.float32
    ).astype(jnp.bfloat16)
    deg_odd = jnp.einsum(
        "nuk,nuc->ukc", south_basis, comb_odd, preferred_element_type=jnp.float32
    ).astype(jnp.bfloat16)
    proj_even = jnp.einsum(
        "nuk,ukc->nuc", north_basis, deg_even, preferred_element_type=jnp.float32
    ).astype(jnp.bfloat16).astype(jnp.float32)
    proj_odd = jnp.einsum(
        "nuk,ukc->nuc", south_basis, deg_odd, preferred_element_type=jnp.float32
    ).astype(jnp.bfloat16).astype(jnp.float32)
    grad_units = jnp.concatenate([proj_even + proj_odd, proj_even - proj_odd], 0).astype(
        jnp.bfloat16
    )
    returned = lax.all_to_all(
        grad_units.reshape(lat_count, lat_rows, units_per_dev * unit_width), "lat", 0, 0, tiled=True
    ).transpose(1, 0, 2).reshape(lat_rows, 2 * wave_dev, width)

    by_pair = returned.reshape(lon_count // 4, 1, 2, pair_rows, 2 * wave_dev, width)
    pair_send = jnp.broadcast_to(
        by_pair, (lon_count // 4, halves, 2, pair_rows, 2 * wave_dev, width)
    ).reshape(lon_count, pair_rows, 2 * wave_dev, width)
    pair_coeffs = lax.all_to_all(pair_send, "lon", 0, 0, tiled=True)
    pair_coeffs = pair_coeffs.transpose(1, 0, 2, 3).reshape(pair_rows, 2 * wave_dev * lon_count, width)
    half_grid = split_dot(table_hi, table_lo, pair_coeffs, (((1,), (1,)), ((), ())))
    half_send = half_grid.astype(jnp.bfloat16).reshape(group, lon_dev, pair_rows, width).transpose(0, 2, 1, 3)
    spatial = lax.all_to_all(
        half_send, "lon", 0, 0, tiled=True, axis_index_groups=half_groups
    ).reshape(lat_rows, lon_dev, width)
    mixed = jnp.einsum("rlc,dc->rld", spatial, spectral_weight, preferred_element_type=jnp.float32)
    return (mixed + skip_term).astype(jnp.bfloat16)


def solution(mesh):
    return jax.shard_map(
        shards,
        mesh=mesh,
        in_specs=(P("lat", "lon", None), P("lat", "lon", None), P(), P()),
        out_specs=P("lat", "lon", None),
        check_vma=False,
    )
```

```python
import math

import numpy as np

import jax
import jax.numpy as jnp
from jax import lax
from jax.sharding import PartitionSpec as P


def fourier_table(block, lon_dev, count_lon, count_wave):
    column = lax.broadcasted_iota(jnp.int32, (1, 2 * count_wave), 1)
    wavenum = column // 2

    def turns(longitude):
        phases = (longitude[:, None] * wavenum) % count_lon
        angles = phases.astype(jnp.float32) * (2.0 * math.pi / count_lon)
        return jnp.cos(angles), jnp.sin(angles)

    block_cos, block_sin = turns(lon_dev * block)
    inner_cos, inner_sin = turns(jnp.arange(lon_dev))
    rows = block.shape[0] * lon_dev
    block_cos, block_sin = (jnp.repeat(t, lon_dev, axis=0) for t in (block_cos, block_sin))
    inner_cos, inner_sin = (jnp.tile(t, (block.shape[0], 1)) for t in (inner_cos, inner_sin))
    cosine = block_cos * inner_cos - block_sin * inner_sin
    sine = block_sin * inner_cos + block_cos * inner_sin
    parity = jnp.broadcast_to(column % 2, (rows, 2 * count_wave))
    table = math.sqrt(2.0 / count_lon) * jnp.where(parity == 0, cosine, -sine)
    high = lax.reduce_precision(table, exponent_bits=8, mantissa_bits=7)
    return lax.optimization_barrier((high.astype(jnp.bfloat16), (table - high).astype(jnp.bfloat16)))


def split_dot(table_hi, table_lo, values, dims):
    dot = lambda t: lax.dot_general(t, values, dims, preferred_element_type=jnp.float32)
    return dot(table_hi) + dot(table_lo)


def unit_slots(lat_count, units_per_dev):
    first = [(units_per_dev * t) // 4 for t in range(lat_count)]
    last = [(units_per_dev * t + units_per_dev - 1) // 4 for t in range(lat_count)]
    return np.stack([np.array(first), np.array(last)], axis=1)


def shards(cotangent, legendre, spectral_weight, skip_weight):
    lat_rows, lon_dev, width = cotangent.shape
    lat_count = lax.axis_size("lat")
    lon_count = lax.axis_size("lon")
    count_lon = lon_dev * lon_count
    wave_dev = legendre.shape[1]
    half_deg = legendre.shape[2]
    all_rows = lat_rows * lat_count
    half_rows = all_rows // 2
    skip_term = jnp.einsum("rlc,dc->rld", cotangent, skip_weight, preferred_element_type=jnp.float32)

    halves = 2
    group = lon_count // halves
    pair_rows = lat_rows // group
    own_half = (lax.axis_index("lon") // 2) % halves
    position = jnp.arange(group)
    block = (position // 2) * 4 + 2 * own_half + position % 2
    table_hi, table_lo = fourier_table(block, lon_dev, count_lon, wave_dev * lon_count)
    lon_ids = np.arange(lon_count).reshape(lon_count // 4, halves, 2)
    half_groups = [lon_ids[:, h, :].reshape(-1).tolist() for h in range(halves)]

    pair_grid = lax.all_to_all(
        cotangent.reshape(group, pair_rows, lon_dev, width), "lon", 0, 0, tiled=True,
        axis_index_groups=half_groups,
    ).transpose(1, 0, 2, 3).reshape(pair_rows, group * lon_dev, width)
    partial = split_dot(table_hi, table_lo, pair_grid, (((0,), (1,)), ((), ())))
    partial_recv = lax.all_to_all(
        partial.astype(jnp.bfloat16).reshape(lon_count, 2 * wave_dev, pair_rows, width), "lon", 0, 0, tiled=True
    ).reshape(lon_count // 4, halves, 2, 2 * wave_dev, pair_rows, width)
    coeffs = jnp.sum(partial_recv.astype(jnp.float32), axis=1).astype(jnp.bfloat16)
    coeffs = coeffs.transpose(0, 1, 3, 2, 4).reshape(lat_rows, 2 * wave_dev, width)
    units_total = wave_dev * 4
    units_per_dev = units_total // lat_count
    unit_width = width // 2
    unit_send = coeffs.reshape(lat_rows, lat_count, units_per_dev * unit_width).transpose(1, 0, 2)
    slots = unit_slots(lat_count, units_per_dev)
    basis_send = jnp.stack(
        [jnp.concatenate([legendre[:, a], legendre[:, b]], axis=-1) for a, b in slots.tolist()]
    )
    payload = jnp.concatenate([unit_send, basis_send], axis=-1)
    arrived = lax.all_to_all(payload, "lat", 0, 0, tiled=True).reshape(all_rows, -1)
    gathered = arrived[:, : units_per_dev * unit_width].reshape(all_rows, units_per_dev, unit_width)
    basis_recv = arrived[:, units_per_dev * unit_width :].reshape(all_rows, 2, half_deg)

    band = lax.axis_index("lat")
    unit_ids = units_per_dev * band + jnp.arange(units_per_dev)
    local_wave = unit_ids // 4
    use_last = (local_wave - (units_per_dev * band) // 4) > 0
    basis = jnp.where(
        use_last[None, :, None], basis_recv[:, 1:2, :], basis_recv[:, 0:1, :]
    )
    wavenum = lax.axis_index("lon") * wave_dev + local_wave
    degree = 2 * jnp.arange(half_deg)
    parity = wavenum % 2
    mask_even = degree[None, :] + parity[:, None] >= wavenum[:, None]
    mask_odd = degree[None, :] + 1 - parity[:, None] >= wavenum[:, None]
    north_basis = jnp.where(mask_even[None], basis[:half_rows], jnp.zeros_like(basis[:half_rows]))
    south_basis = jnp.where(mask_odd[None], basis[half_rows:], jnp.zeros_like(basis[half_rows:]))

    north_wide = gathered[:half_rows].astype(jnp.float32)
    south_wide = gathered[half_rows:].astype(jnp.float32)
    comb_even = (north_wide + south_wide).astype(jnp.bfloat16)
    comb_odd = (north_wide - south_wide).astype(jnp.bfloat16)
    deg_even = jnp.einsum(
        "nuk,nuc->ukc", north_basis, comb_even, preferred_element_type=jnp.float32
    ).astype(jnp.bfloat16)
    deg_odd = jnp.einsum(
        "nuk,nuc->ukc", south_basis, comb_odd, preferred_element_type=jnp.float32
    ).astype(jnp.bfloat16)
    proj_even = jnp.einsum(
        "nuk,ukc->nuc", north_basis, deg_even, preferred_element_type=jnp.float32
    ).astype(jnp.bfloat16).astype(jnp.float32)
    proj_odd = jnp.einsum(
        "nuk,ukc->nuc", south_basis, deg_odd, preferred_element_type=jnp.float32
    ).astype(jnp.bfloat16).astype(jnp.float32)
    grad_units = jnp.concatenate([proj_even + proj_odd, proj_even - proj_odd], 0).astype(
        jnp.bfloat16
    )
    returned = lax.all_to_all(
        grad_units.reshape(lat_count, lat_rows, units_per_dev * unit_width), "lat", 0, 0, tiled=True
    ).transpose(1, 0, 2).reshape(lat_rows, 2 * wave_dev, width)

    by_pair = returned.reshape(lon_count // 4, 1, 2, pair_rows, 2 * wave_dev, width)
    pair_send = jnp.broadcast_to(
        by_pair, (lon_count // 4, halves, 2, pair_rows, 2 * wave_dev, width)
    ).reshape(lon_count, pair_rows, 2 * wave_dev, width)
    pair_coeffs = lax.all_to_all(pair_send, "lon", 0, 0, tiled=True)
    pair_coeffs = pair_coeffs.transpose(1, 0, 2, 3).reshape(pair_rows, 2 * wave_dev * lon_count, width)
    half_grid = split_dot(table_hi, table_lo, pair_coeffs, (((1,), (1,)), ((), ())))
    half_send = half_grid.astype(jnp.bfloat16).reshape(group, lon_dev, pair_rows, width).transpose(0, 2, 1, 3)
    spatial = lax.all_to_all(
        half_send, "lon", 0, 0, tiled=True, axis_index_groups=half_groups
    ).reshape(lat_rows, lon_dev, width)
    mixed = jnp.einsum("rlc,dc->rld", spatial, spectral_weight, preferred_element_type=jnp.float32)
    return (mixed + skip_term).astype(jnp.bfloat16)


def solution(mesh):
    return jax.shard_map(
        shards,
        mesh=mesh,
        in_specs=(P("lat", "lon", None), P("lat", "lon", None), P(), P()),
        out_specs=P("lat", "lon", None),
        check_vma=False,
    )
```

```python
import math

import numpy as np

import jax
import jax.numpy as jnp
from jax import lax
from jax.sharding import PartitionSpec as P


def fourier_table(longitude, count_lon, count_wave):
    column = lax.broadcasted_iota(jnp.int32, (longitude.shape[0], 2 * count_wave), 1)
    phases = (longitude[:, None] * (column // 2) + (count_lon // 4) * (column % 2)) % count_lon
    angles = phases.astype(jnp.float32) * (2.0 * math.pi / count_lon)
    table = math.sqrt(2.0 / count_lon) * jnp.cos(angles)
    high = lax.reduce_precision(table, exponent_bits=8, mantissa_bits=7)
    return lax.optimization_barrier((high.astype(jnp.bfloat16), (table - high).astype(jnp.bfloat16)))


def split_dot(table_hi, table_lo, values, dims):
    dot = lambda t: lax.dot_general(t, values, dims, preferred_element_type=jnp.float32)
    return dot(table_hi) + dot(table_lo)


def unit_slots(lat_count, units_per_dev):
    first = [(units_per_dev * t) // 4 for t in range(lat_count)]
    last = [(units_per_dev * t + units_per_dev - 1) // 4 for t in range(lat_count)]
    return np.stack([np.array(first), np.array(last)], axis=1)


def shards(cotangent, legendre, spectral_weight, skip_weight):
    lat_rows, lon_dev, width = cotangent.shape
    lat_count = lax.axis_size("lat")
    lon_count = lax.axis_size("lon")
    count_lon = lon_dev * lon_count
    wave_dev = legendre.shape[1]
    half_deg = legendre.shape[2]
    all_rows = lat_rows * lat_count
    half_rows = all_rows // 2
    skip_term = jnp.einsum("rlc,dc->rld", cotangent, skip_weight, preferred_element_type=jnp.float32)

    halves = 2
    group = lon_count // halves
    pair_rows = lat_rows // group
    own_half = (lax.axis_index("lon") // 2) % halves
    position = jnp.arange(group * lon_dev) // lon_dev
    longitude = lon_dev * ((position // 2) * 4 + 2 * own_half + position % 2) + jnp.arange(
        group * lon_dev
    ) % lon_dev
    table_hi, table_lo = fourier_table(longitude, count_lon, wave_dev * lon_count)
    lon_ids = np.arange(lon_count).reshape(lon_count // 4, halves, 2)
    half_groups = [lon_ids[:, h, :].reshape(-1).tolist() for h in range(halves)]

    pair_grid = lax.all_to_all(
        cotangent.reshape(group, pair_rows * lon_dev, width), "lon", 0, 0, tiled=True,
        axis_index_groups=half_groups,
    ).reshape(group, pair_rows, lon_dev, width).transpose(1, 0, 2, 3).reshape(pair_rows, group * lon_dev, width)
    partial = split_dot(table_hi, table_lo, pair_grid, (((0,), (1,)), ((), ())))
    partial_recv = lax.all_to_all(
        partial.astype(jnp.bfloat16).reshape(lon_count, 2 * wave_dev, pair_rows, width), "lon", 0, 0, tiled=True
    ).reshape(lon_count // 4, halves, 2, 2 * wave_dev, pair_rows, width)
    coeffs = jnp.sum(partial_recv.astype(jnp.float32), axis=1).astype(jnp.bfloat16)
    coeffs = coeffs.transpose(0, 1, 3, 2, 4).reshape(lat_rows, 2 * wave_dev, width)
    units_total = wave_dev * 4
    units_per_dev = units_total // lat_count
    unit_width = width // 2
    unit_send = coeffs.reshape(lat_rows, lat_count, units_per_dev * unit_width).transpose(1, 0, 2)
    slots = unit_slots(lat_count, units_per_dev)
    basis_send = jnp.stack(
        [jnp.concatenate([legendre[:, a], legendre[:, b]], axis=-1) for a, b in slots.tolist()]
    )
    payload = jnp.concatenate([unit_send, basis_send], axis=-1)
    arrived = lax.all_to_all(payload, "lat", 0, 0, tiled=True).reshape(all_rows, -1)
    gathered = arrived[:, : units_per_dev * unit_width].reshape(all_rows, units_per_dev, unit_width)
    basis_recv = arrived[:, units_per_dev * unit_width :].reshape(all_rows, 2, half_deg)

    band = lax.axis_index("lat")
    unit_ids = units_per_dev * band + jnp.arange(units_per_dev)
    local_wave = unit_ids // 4
    use_last = (local_wave - (units_per_dev * band) // 4) > 0
    basis = jnp.where(
        use_last[None, :, None], basis_recv[:, 1:2, :], basis_recv[:, 0:1, :]
    )
    wavenum = lax.axis_index("lon") * wave_dev + local_wave
    degree = 2 * jnp.arange(half_deg)
    parity = wavenum % 2
    mask_even = degree[None, :] + parity[:, None] >= wavenum[:, None]
    mask_odd = degree[None, :] + 1 - parity[:, None] >= wavenum[:, None]
    north_basis = jnp.where(mask_even[None], basis[:half_rows], jnp.zeros_like(basis[:half_rows]))
    south_basis = jnp.where(mask_odd[None], basis[half_rows:], jnp.zeros_like(basis[half_rows:]))

    north_wide = gathered[:half_rows].astype(jnp.float32)
    south_wide = gathered[half_rows:].astype(jnp.float32)
    comb_even = (north_wide + south_wide).astype(jnp.bfloat16)
    comb_odd = (north_wide - south_wide).astype(jnp.bfloat16)
    deg_even = jnp.einsum(
        "nuk,nuc->ukc", north_basis, comb_even, preferred_element_type=jnp.float32
    ).astype(jnp.bfloat16)
    deg_odd = jnp.einsum(
        "nuk,nuc->ukc", south_basis, comb_odd, preferred_element_type=jnp.float32
    ).astype(jnp.bfloat16)
    proj_even = jnp.einsum(
        "nuk,ukc->nuc", north_basis, deg_even, preferred_element_type=jnp.float32
    ).astype(jnp.bfloat16).astype(jnp.float32)
    proj_odd = jnp.einsum(
        "nuk,ukc->nuc", south_basis, deg_odd, preferred_element_type=jnp.float32
    ).astype(jnp.bfloat16).astype(jnp.float32)
    grad_units = jnp.concatenate([proj_even + proj_odd, proj_even - proj_odd], 0).astype(
        jnp.bfloat16
    )
    returned = lax.all_to_all(
        grad_units.reshape(lat_count, lat_rows, units_per_dev * unit_width), "lat", 0, 0, tiled=True
    ).transpose(1, 0, 2).reshape(lat_rows, 2 * wave_dev, width)

    by_pair = returned.reshape(lon_count // 4, 1, 2, pair_rows, 2 * wave_dev, width)
    pair_send = jnp.broadcast_to(
        by_pair, (lon_count // 4, halves, 2, pair_rows, 2 * wave_dev, width)
    ).reshape(lon_count, pair_rows, 2 * wave_dev, width)
    pair_coeffs = lax.all_to_all(pair_send, "lon", 0, 0, tiled=True)
    pair_coeffs = pair_coeffs.transpose(1, 0, 2, 3).reshape(pair_rows, 2 * wave_dev * lon_count, width)
    half_grid = split_dot(table_hi, table_lo, pair_coeffs, (((1,), (1,)), ((), ())))
    half_send = half_grid.astype(jnp.bfloat16).reshape(group, lon_dev, pair_rows, width).transpose(0, 2, 1, 3)
    half_send = half_send.reshape(group, pair_rows * lon_dev, width)
    spatial = lax.all_to_all(
        half_send, "lon", 0, 0, tiled=True, axis_index_groups=half_groups
    ).reshape(lat_rows, lon_dev, width)
    mixed = jnp.einsum("rlc,dc->rld", spatial, spectral_weight, preferred_element_type=jnp.float32)
    return (mixed + skip_term).astype(jnp.bfloat16)


def solution(mesh):
    return jax.shard_map(
        shards,
        mesh=mesh,
        in_specs=(P("lat", "lon", None), P("lat", "lon", None), P(), P()),
        out_specs=P("lat", "lon", None),
        check_vma=False,
    )
```

```python
import math

import numpy as np

import jax
import jax.numpy as jnp
from jax import lax
from jax.sharding import PartitionSpec as P


def fourier_table(longitude, count_lon, count_wave):
    column = lax.broadcasted_iota(jnp.int32, (longitude.shape[0], 2 * count_wave), 1)
    phases = (longitude[:, None] * (column // 2) + (count_lon // 4) * (column % 2)) % count_lon
    angles = phases.astype(jnp.float32) * (2.0 * math.pi / count_lon)
    table = math.sqrt(2.0 / count_lon) * jnp.cos(angles)
    high = lax.reduce_precision(table, exponent_bits=8, mantissa_bits=7)
    return lax.optimization_barrier((high.astype(jnp.bfloat16), (table - high).astype(jnp.bfloat16)))


def split_dot(table_hi, table_lo, values, dims):
    dot = lambda t: lax.dot_general(t, values, dims, preferred_element_type=jnp.float32)
    return dot(table_hi) + dot(table_lo)


def unit_slots(lat_count, units_per_dev):
    first = [(units_per_dev * t) // 4 for t in range(lat_count)]
    last = [(units_per_dev * t + units_per_dev - 1) // 4 for t in range(lat_count)]
    return np.stack([np.array(first), np.array(last)], axis=1)


def shards(cotangent, legendre, spectral_weight, skip_weight):
    lat_rows, lon_dev, width = cotangent.shape
    lat_count = lax.axis_size("lat")
    lon_count = lax.axis_size("lon")
    count_lon = lon_dev * lon_count
    wave_dev = legendre.shape[1]
    half_deg = legendre.shape[2]
    all_rows = lat_rows * lat_count
    half_rows = all_rows // 2
    skip_term = jnp.einsum("rlc,dc->rld", cotangent, skip_weight, preferred_element_type=jnp.float32)

    halves = 2
    group = lon_count // halves
    pair_rows = lat_rows // group
    own_half = (lax.axis_index("lon") // 2) % halves
    position = jnp.arange(group * lon_dev) // lon_dev
    longitude = lon_dev * ((position // 2) * 4 + 2 * own_half + position % 2) + jnp.arange(
        group * lon_dev
    ) % lon_dev
    table_hi, table_lo = fourier_table(longitude, count_lon, wave_dev * lon_count)
    lon_ids = np.arange(lon_count).reshape(lon_count // 4, halves, 2)
    half_groups = [lon_ids[:, h, :].reshape(-1).tolist() for h in range(halves)]

    pair_grid = lax.all_to_all(
        cotangent.reshape(group, pair_rows * lon_dev, width), "lon", 0, 0, tiled=True,
        axis_index_groups=half_groups,
    ).reshape(group, pair_rows, lon_dev, width)
    partial = split_dot(
        table_hi.reshape(group, lon_dev, -1), table_lo.reshape(group, lon_dev, -1), pair_grid,
        (((0, 1), (0, 2)), ((), ())),
    )
    partial_recv = lax.all_to_all(
        partial.astype(jnp.bfloat16).reshape(lon_count, 2 * wave_dev, pair_rows, width), "lon", 0, 0, tiled=True
    ).reshape(lon_count // 4, halves, 2, 2 * wave_dev, pair_rows, width)
    coeffs = jnp.sum(partial_recv.astype(jnp.float32), axis=1).astype(jnp.bfloat16)
    coeffs = coeffs.transpose(0, 1, 3, 2, 4).reshape(lat_rows, 2 * wave_dev, width)
    units_total = wave_dev * 4
    units_per_dev = units_total // lat_count
    unit_width = width // 2
    unit_send = coeffs.reshape(lat_rows, lat_count, units_per_dev * unit_width).transpose(1, 0, 2)
    slots = unit_slots(lat_count, units_per_dev)
    basis_send = jnp.stack(
        [jnp.concatenate([legendre[:, a], legendre[:, b]], axis=-1) for a, b in slots.tolist()]
    )
    payload = jnp.concatenate([unit_send, basis_send], axis=-1)
    arrived = lax.all_to_all(payload, "lat", 0, 0, tiled=True).reshape(all_rows, -1)
    gathered = arrived[:, : units_per_dev * unit_width].reshape(all_rows, units_per_dev, unit_width)
    basis_recv = arrived[:, units_per_dev * unit_width :].reshape(all_rows, 2, half_deg)

    band = lax.axis_index("lat")
    unit_ids = units_per_dev * band + jnp.arange(units_per_dev)
    local_wave = unit_ids // 4
    use_last = (local_wave - (units_per_dev * band) // 4) > 0
    basis = jnp.where(
        use_last[None, :, None], basis_recv[:, 1:2, :], basis_recv[:, 0:1, :]
    )
    wavenum = lax.axis_index("lon") * wave_dev + local_wave
    degree = 2 * jnp.arange(half_deg)
    parity = wavenum % 2
    mask_even = degree[None, :] + parity[:, None] >= wavenum[:, None]
    mask_odd = degree[None, :] + 1 - parity[:, None] >= wavenum[:, None]
    north_basis = jnp.where(mask_even[None], basis[:half_rows], jnp.zeros_like(basis[:half_rows]))
    south_basis = jnp.where(mask_odd[None], basis[half_rows:], jnp.zeros_like(basis[half_rows:]))

    north_wide = gathered[:half_rows].astype(jnp.float32)
    south_wide = gathered[half_rows:].astype(jnp.float32)
    comb_even = (north_wide + south_wide).astype(jnp.bfloat16)
    comb_odd = (north_wide - south_wide).astype(jnp.bfloat16)
    deg_even = jnp.einsum(
        "nuk,nuc->ukc", north_basis, comb_even, preferred_element_type=jnp.float32
    ).astype(jnp.bfloat16)
    deg_odd = jnp.einsum(
        "nuk,nuc->ukc", south_basis, comb_odd, preferred_element_type=jnp.float32
    ).astype(jnp.bfloat16)
    proj_even = jnp.einsum(
        "nuk,ukc->nuc", north_basis, deg_even, preferred_element_type=jnp.float32
    ).astype(jnp.bfloat16).astype(jnp.float32)
    proj_odd = jnp.einsum(
        "nuk,ukc->nuc", south_basis, deg_odd, preferred_element_type=jnp.float32
    ).astype(jnp.bfloat16).astype(jnp.float32)
    grad_units = jnp.concatenate([proj_even + proj_odd, proj_even - proj_odd], 0).astype(
        jnp.bfloat16
    )
    returned = lax.all_to_all(
        grad_units.reshape(lat_count, lat_rows, units_per_dev * unit_width), "lat", 0, 0, tiled=True
    ).transpose(1, 0, 2).reshape(lat_rows, 2 * wave_dev, width)

    by_pair = returned.reshape(lon_count // 4, 1, 2, pair_rows, 2 * wave_dev, width)
    pair_send = jnp.broadcast_to(
        by_pair, (lon_count // 4, halves, 2, pair_rows, 2 * wave_dev, width)
    ).reshape(lon_count, pair_rows, 2 * wave_dev, width)
    pair_coeffs = lax.all_to_all(pair_send, "lon", 0, 0, tiled=True)
    pair_coeffs = pair_coeffs.transpose(1, 0, 2, 3).reshape(pair_rows, 2 * wave_dev * lon_count, width)
    half_grid = split_dot(table_hi, table_lo, pair_coeffs, (((1,), (1,)), ((), ())))
    half_send = half_grid.astype(jnp.bfloat16).reshape(group, lon_dev, pair_rows, width).transpose(0, 2, 1, 3)
    half_send = half_send.reshape(group, pair_rows * lon_dev, width)
    spatial = lax.all_to_all(
        half_send, "lon", 0, 0, tiled=True, axis_index_groups=half_groups
    ).reshape(lat_rows, lon_dev, width)
    mixed = jnp.einsum("rlc,dc->rld", spatial, spectral_weight, preferred_element_type=jnp.float32)
    return (mixed + skip_term).astype(jnp.bfloat16)


def solution(mesh):
    return jax.shard_map(
        shards,
        mesh=mesh,
        in_specs=(P("lat", "lon", None), P("lat", "lon", None), P(), P()),
        out_specs=P("lat", "lon", None),
        check_vma=False,
    )
```

```python
import math

import numpy as np

import jax
import jax.numpy as jnp
from jax import lax
from jax.sharding import PartitionSpec as P


def fourier_table(longitude, count_lon, count_wave):
    column = lax.broadcasted_iota(jnp.int32, (longitude.shape[0], 2 * count_wave), 1)
    phases = (longitude[:, None] * (column // 2) + (count_lon // 4) * (column % 2)) % count_lon
    angles = phases.astype(jnp.float32) * (2.0 * math.pi / count_lon)
    table = math.sqrt(2.0 / count_lon) * jnp.cos(angles)
    return lax.optimization_barrier(table.astype(jnp.bfloat16))


def table_dot(table, values, dims):
    return lax.dot_general(table, values, dims, preferred_element_type=jnp.float32)


def unit_slots(lat_count, units_per_dev):
    first = [(units_per_dev * t) // 4 for t in range(lat_count)]
    last = [(units_per_dev * t + units_per_dev - 1) // 4 for t in range(lat_count)]
    return np.stack([np.array(first), np.array(last)], axis=1)


def shards(cotangent, legendre, spectral_weight, skip_weight):
    lat_rows, lon_dev, width = cotangent.shape
    lat_count = lax.axis_size("lat")
    lon_count = lax.axis_size("lon")
    count_lon = lon_dev * lon_count
    wave_dev = legendre.shape[1]
    half_deg = legendre.shape[2]
    all_rows = lat_rows * lat_count
    half_rows = all_rows // 2
    skip_term = jnp.einsum("rlc,dc->rld", cotangent, skip_weight, preferred_element_type=jnp.float32)

    halves = 2
    group = lon_count // halves
    pair_rows = lat_rows // group
    own_half = (lax.axis_index("lon") // 2) % halves
    position = jnp.arange(group * lon_dev) // lon_dev
    longitude = lon_dev * ((position // 2) * 4 + 2 * own_half + position % 2) + jnp.arange(
        group * lon_dev
    ) % lon_dev
    table = fourier_table(longitude, count_lon, wave_dev * lon_count)
    lon_ids = np.arange(lon_count).reshape(lon_count // 4, halves, 2)
    half_groups = [lon_ids[:, h, :].reshape(-1).tolist() for h in range(halves)]

    pair_grid = lax.all_to_all(
        cotangent.reshape(group, pair_rows * lon_dev, width), "lon", 0, 0, tiled=True,
        axis_index_groups=half_groups,
    ).reshape(group, pair_rows, lon_dev, width).transpose(1, 0, 2, 3).reshape(pair_rows, group * lon_dev, width)
    partial = table_dot(table, pair_grid, (((0,), (1,)), ((), ())))
    partial_recv = lax.all_to_all(
        partial.astype(jnp.bfloat16).reshape(lon_count, 2 * wave_dev, pair_rows, width), "lon", 0, 0, tiled=True
    ).reshape(lon_count // 4, halves, 2, 2 * wave_dev, pair_rows, width)
    coeffs = jnp.sum(partial_recv.astype(jnp.float32), axis=1).astype(jnp.bfloat16)
    coeffs = coeffs.transpose(0, 1, 3, 2, 4).reshape(lat_rows, 2 * wave_dev, width)
    units_total = wave_dev * 4
    units_per_dev = units_total // lat_count
    unit_width = width // 2
    unit_send = coeffs.reshape(lat_rows, lat_count, units_per_dev * unit_width).transpose(1, 0, 2)
    slots = unit_slots(lat_count, units_per_dev)
    basis_send = jnp.stack(
        [jnp.concatenate([legendre[:, a], legendre[:, b]], axis=-1) for a, b in slots.tolist()]
    )
    payload = jnp.concatenate([unit_send, basis_send], axis=-1)
    arrived = lax.all_to_all(payload, "lat", 0, 0, tiled=True).reshape(all_rows, -1)
    gathered = arrived[:, : units_per_dev * unit_width].reshape(all_rows, units_per_dev, unit_width)
    basis_recv = arrived[:, units_per_dev * unit_width :].reshape(all_rows, 2, half_deg)

    band = lax.axis_index("lat")
    unit_ids = units_per_dev * band + jnp.arange(units_per_dev)
    local_wave = unit_ids // 4
    use_last = (local_wave - (units_per_dev * band) // 4) > 0
    basis = jnp.where(
        use_last[None, :, None], basis_recv[:, 1:2, :], basis_recv[:, 0:1, :]
    )
    wavenum = lax.axis_index("lon") * wave_dev + local_wave
    degree = 2 * jnp.arange(half_deg)
    parity = wavenum % 2
    mask_even = degree[None, :] + parity[:, None] >= wavenum[:, None]
    mask_odd = degree[None, :] + 1 - parity[:, None] >= wavenum[:, None]
    north_basis = jnp.where(mask_even[None], basis[:half_rows], jnp.zeros_like(basis[:half_rows]))
    south_basis = jnp.where(mask_odd[None], basis[half_rows:], jnp.zeros_like(basis[half_rows:]))

    north_wide = gathered[:half_rows].astype(jnp.float32)
    south_wide = gathered[half_rows:].astype(jnp.float32)
    comb_even = (north_wide + south_wide).astype(jnp.bfloat16)
    comb_odd = (north_wide - south_wide).astype(jnp.bfloat16)
    deg_even = jnp.einsum(
        "nuk,nuc->ukc", north_basis, comb_even, preferred_element_type=jnp.float32
    ).astype(jnp.bfloat16)
    deg_odd = jnp.einsum(
        "nuk,nuc->ukc", south_basis, comb_odd, preferred_element_type=jnp.float32
    ).astype(jnp.bfloat16)
    proj_even = jnp.einsum(
        "nuk,ukc->nuc", north_basis, deg_even, preferred_element_type=jnp.float32
    ).astype(jnp.bfloat16).astype(jnp.float32)
    proj_odd = jnp.einsum(
        "nuk,ukc->nuc", south_basis, deg_odd, preferred_element_type=jnp.float32
    ).astype(jnp.bfloat16).astype(jnp.float32)
    grad_units = jnp.concatenate([proj_even + proj_odd, proj_even - proj_odd], 0).astype(
        jnp.bfloat16
    )
    returned = lax.all_to_all(
        grad_units.reshape(lat_count, lat_rows, units_per_dev * unit_width), "lat", 0, 0, tiled=True
    ).transpose(1, 0, 2).reshape(lat_rows, 2 * wave_dev, width)

    by_pair = returned.reshape(lon_count // 4, 1, 2, pair_rows, 2 * wave_dev, width)
    pair_send = jnp.broadcast_to(
        by_pair, (lon_count // 4, halves, 2, pair_rows, 2 * wave_dev, width)
    ).reshape(lon_count, pair_rows, 2 * wave_dev, width)
    pair_coeffs = lax.all_to_all(pair_send, "lon", 0, 0, tiled=True)
    pair_coeffs = pair_coeffs.transpose(1, 0, 2, 3).reshape(pair_rows, 2 * wave_dev * lon_count, width)
    half_grid = table_dot(table, pair_coeffs, (((1,), (1,)), ((), ())))
    half_send = half_grid.astype(jnp.bfloat16).reshape(group, lon_dev, pair_rows, width).transpose(0, 2, 1, 3)
    half_send = half_send.reshape(group, pair_rows * lon_dev, width)
    spatial = lax.all_to_all(
        half_send, "lon", 0, 0, tiled=True, axis_index_groups=half_groups
    ).reshape(lat_rows, lon_dev, width)
    mixed = jnp.einsum("rlc,dc->rld", spatial, spectral_weight, preferred_element_type=jnp.float32)
    return (mixed + skip_term).astype(jnp.bfloat16)


def solution(mesh):
    return jax.shard_map(
        shards,
        mesh=mesh,
        in_specs=(P("lat", "lon", None), P("lat", "lon", None), P(), P()),
        out_specs=P("lat", "lon", None),
        check_vma=False,
    )
```

```python
import math

import numpy as np

import jax
import jax.numpy as jnp
from jax import lax
from jax.sharding import PartitionSpec as P


def fourier_table(longitude, count_lon, count_wave):
    column = lax.broadcasted_iota(jnp.int32, (longitude.shape[0], 2 * count_wave), 1)
    phases = (longitude[:, None] * (column // 2) + (count_lon // 4) * (column % 2)) % count_lon
    angles = phases.astype(jnp.float32) * (2.0 * math.pi / count_lon)
    table = math.sqrt(2.0 / count_lon) * jnp.cos(angles)
    return lax.optimization_barrier(table.astype(jnp.bfloat16))


def table_dot(table, values, dims):
    return lax.dot_general(table, values, dims, preferred_element_type=jnp.float32)


def unit_slots(lat_count, units_per_dev):
    first = [(units_per_dev * t) // 4 for t in range(lat_count)]
    last = [(units_per_dev * t + units_per_dev - 1) // 4 for t in range(lat_count)]
    return np.stack([np.array(first), np.array(last)], axis=1)


def shards(cotangent, legendre, spectral_weight, skip_weight):
    lat_rows, lon_dev, width = cotangent.shape
    lat_count = lax.axis_size("lat")
    lon_count = lax.axis_size("lon")
    count_lon = lon_dev * lon_count
    wave_dev = legendre.shape[1]
    half_deg = legendre.shape[2]
    all_rows = lat_rows * lat_count
    half_rows = all_rows // 2
    skip_term = jnp.einsum("rlc,dc->rld", cotangent, skip_weight, preferred_element_type=jnp.float32)

    halves = 2
    group = lon_count // halves
    pair_rows = lat_rows // group
    own_half = (lax.axis_index("lon") // 2) % halves
    position = jnp.arange(group * lon_dev) // lon_dev
    longitude = lon_dev * ((position // 2) * 4 + 2 * own_half + position % 2) + jnp.arange(
        group * lon_dev
    ) % lon_dev
    table = fourier_table(longitude, count_lon, wave_dev * lon_count)
    lon_ids = np.arange(lon_count).reshape(lon_count // 4, halves, 2)
    half_groups = [lon_ids[:, h, :].reshape(-1).tolist() for h in range(halves)]

    pair_grid = lax.all_to_all(
        cotangent.reshape(group, pair_rows * lon_dev, width), "lon", 0, 0, tiled=True,
        axis_index_groups=half_groups,
    ).reshape(group, pair_rows, lon_dev, width).transpose(1, 0, 2, 3).reshape(pair_rows, group * lon_dev, width)
    partial = table_dot(table, pair_grid, (((0,), (1,)), ((), ())))
    partial_recv = lax.all_to_all(
        partial.astype(jnp.bfloat16).reshape(lon_count, 2 * wave_dev, pair_rows, width), "lon", 0, 0, tiled=True
    ).reshape(lon_count // 4, halves, 2, 2 * wave_dev, pair_rows, width)
    units_total = wave_dev * 4
    units_per_dev = units_total // lat_count
    unit_width = width // 2
    summed = jnp.sum(partial_recv.astype(jnp.float32), axis=1).astype(jnp.bfloat16)
    summed = summed.reshape(lon_count // 4, 2, 2 * wave_dev, pair_rows, 2, unit_width)
    unit_send = summed.transpose(2, 4, 0, 1, 3, 5).reshape(
        lat_count, units_per_dev, lat_rows, unit_width
    ).transpose(0, 2, 1, 3).reshape(lat_count, lat_rows, units_per_dev * unit_width)
    slots = unit_slots(lat_count, units_per_dev)
    basis_send = jnp.stack(
        [jnp.concatenate([legendre[:, a], legendre[:, b]], axis=-1) for a, b in slots.tolist()]
    )
    payload = jnp.concatenate([unit_send, basis_send], axis=-1)
    arrived = lax.all_to_all(payload, "lat", 0, 0, tiled=True).reshape(all_rows, -1)
    gathered = arrived[:, : units_per_dev * unit_width].reshape(all_rows, units_per_dev, unit_width)
    basis_recv = arrived[:, units_per_dev * unit_width :].reshape(all_rows, 2, half_deg)

    band = lax.axis_index("lat")
    unit_ids = units_per_dev * band + jnp.arange(units_per_dev)
    local_wave = unit_ids // 4
    use_last = (local_wave - (units_per_dev * band) // 4) > 0
    basis = jnp.where(
        use_last[None, :, None], basis_recv[:, 1:2, :], basis_recv[:, 0:1, :]
    )
    wavenum = lax.axis_index("lon") * wave_dev + local_wave
    degree = 2 * jnp.arange(half_deg)
    parity = wavenum % 2
    mask_even = degree[None, :] + parity[:, None] >= wavenum[:, None]
    mask_odd = degree[None, :] + 1 - parity[:, None] >= wavenum[:, None]
    north_basis = jnp.where(mask_even[None], basis[:half_rows], jnp.zeros_like(basis[:half_rows]))
    south_basis = jnp.where(mask_odd[None], basis[half_rows:], jnp.zeros_like(basis[half_rows:]))

    north_wide = gathered[:half_rows].astype(jnp.float32)
    south_wide = gathered[half_rows:].astype(jnp.float32)
    comb_even = (north_wide + south_wide).astype(jnp.bfloat16)
    comb_odd = (north_wide - south_wide).astype(jnp.bfloat16)
    deg_even = jnp.einsum(
        "nuk,nuc->ukc", north_basis, comb_even, preferred_element_type=jnp.float32
    ).astype(jnp.bfloat16)
    deg_odd = jnp.einsum(
        "nuk,nuc->ukc", south_basis, comb_odd, preferred_element_type=jnp.float32
    ).astype(jnp.bfloat16)
    proj_even = jnp.einsum(
        "nuk,ukc->nuc", north_basis, deg_even, preferred_element_type=jnp.float32
    ).astype(jnp.bfloat16).astype(jnp.float32)
    proj_odd = jnp.einsum(
        "nuk,ukc->nuc", south_basis, deg_odd, preferred_element_type=jnp.float32
    ).astype(jnp.bfloat16).astype(jnp.float32)
    grad_units = jnp.concatenate([proj_even + proj_odd, proj_even - proj_odd], 0).astype(
        jnp.bfloat16
    )
    returned = lax.all_to_all(
        grad_units.reshape(lat_count, lat_rows, units_per_dev * unit_width), "lat", 0, 0, tiled=True
    ).transpose(1, 0, 2).reshape(lat_rows, 2 * wave_dev, width)

    by_pair = returned.reshape(lon_count // 4, 1, 2, pair_rows, 2 * wave_dev, width)
    pair_send = jnp.broadcast_to(
        by_pair, (lon_count // 4, halves, 2, pair_rows, 2 * wave_dev, width)
    ).reshape(lon_count, pair_rows, 2 * wave_dev, width)
    pair_coeffs = lax.all_to_all(pair_send, "lon", 0, 0, tiled=True)
    pair_coeffs = pair_coeffs.transpose(1, 0, 2, 3).reshape(pair_rows, 2 * wave_dev * lon_count, width)
    half_grid = table_dot(table, pair_coeffs, (((1,), (1,)), ((), ())))
    half_send = half_grid.astype(jnp.bfloat16).reshape(group, lon_dev, pair_rows, width).transpose(0, 2, 1, 3)
    half_send = half_send.reshape(group, pair_rows * lon_dev, width)
    spatial = lax.all_to_all(
        half_send, "lon", 0, 0, tiled=True, axis_index_groups=half_groups
    ).reshape(lat_rows, lon_dev, width)
    mixed = jnp.einsum("rlc,dc->rld", spatial, spectral_weight, preferred_element_type=jnp.float32)
    return (mixed + skip_term).astype(jnp.bfloat16)


def solution(mesh):
    return jax.shard_map(
        shards,
        mesh=mesh,
        in_specs=(P("lat", "lon", None), P("lat", "lon", None), P(), P()),
        out_specs=P("lat", "lon", None),
        check_vma=False,
    )
```

```python
import math

import numpy as np

import jax
import jax.numpy as jnp
from jax import lax
from jax.sharding import PartitionSpec as P


def fourier_table(longitude, count_lon, count_wave):
    column = lax.broadcasted_iota(jnp.int32, (longitude.shape[0], 2 * count_wave), 1)
    phases = (longitude[:, None] * (column // 2) + (count_lon // 4) * (column % 2)) % count_lon
    angles = phases.astype(jnp.float32) * (2.0 * math.pi / count_lon)
    table = math.sqrt(2.0 / count_lon) * jnp.cos(angles)
    return lax.optimization_barrier(table.astype(jnp.bfloat16))


def table_dot(table, values, dims):
    return lax.dot_general(table, values, dims, preferred_element_type=jnp.float32)


def unit_slots(lat_count, units_per_dev):
    first = [(units_per_dev * t) // 4 for t in range(lat_count)]
    last = [(units_per_dev * t + units_per_dev - 1) // 4 for t in range(lat_count)]
    return np.stack([np.array(first), np.array(last)], axis=1)


def shards(cotangent, legendre, spectral_weight, skip_weight):
    lat_rows, lon_dev, width = cotangent.shape
    lat_count = lax.axis_size("lat")
    lon_count = lax.axis_size("lon")
    count_lon = lon_dev * lon_count
    wave_dev = legendre.shape[1]
    half_deg = legendre.shape[2]
    all_rows = lat_rows * lat_count
    half_rows = all_rows // 2
    skip_term = jnp.einsum("rlc,dc->rld", cotangent, skip_weight, preferred_element_type=jnp.float32)

    halves = 2
    group = lon_count // halves
    pair_rows = lat_rows // group
    own_half = (lax.axis_index("lon") // 2) % halves
    position = jnp.arange(group * lon_dev) // lon_dev
    longitude = lon_dev * ((position // 2) * 4 + 2 * own_half + position % 2) + jnp.arange(
        group * lon_dev
    ) % lon_dev
    table = fourier_table(longitude, count_lon, wave_dev * lon_count)
    lon_ids = np.arange(lon_count).reshape(lon_count // 4, halves, 2)
    half_groups = [lon_ids[:, h, :].reshape(-1).tolist() for h in range(halves)]

    pair_grid = lax.all_to_all(
        cotangent.reshape(group, pair_rows * lon_dev, width), "lon", 0, 0, tiled=True,
        axis_index_groups=half_groups,
    ).reshape(group, pair_rows, lon_dev, width).transpose(1, 0, 2, 3).reshape(pair_rows, group * lon_dev, width)
    partial = table_dot(table, pair_grid, (((0,), (1,)), ((), ())))
    partial_recv = lax.all_to_all(
        partial.astype(jnp.bfloat16).reshape(lon_count, 2 * wave_dev, pair_rows, width), "lon", 0, 0, tiled=True
    ).reshape(lon_count // 4, halves, 2, 2 * wave_dev, pair_rows, width)
    coeffs = jnp.sum(partial_recv.astype(jnp.float32), axis=1).astype(jnp.bfloat16)
    coeffs = coeffs.transpose(0, 1, 3, 2, 4).reshape(lat_rows, 2 * wave_dev, width)
    units_total = wave_dev * 4
    units_per_dev = units_total // lat_count
    unit_width = width // 2
    unit_send = coeffs.reshape(lat_rows, lat_count, units_per_dev * unit_width).transpose(1, 0, 2)
    slots = unit_slots(lat_count, units_per_dev)
    basis_send = jnp.stack(
        [jnp.concatenate([legendre[:, a], legendre[:, b]], axis=-1) for a, b in slots.tolist()]
    )
    payload = jnp.concatenate([unit_send, basis_send], axis=-1)
    arrived = lax.all_to_all(payload, "lat", 0, 0, tiled=True).reshape(all_rows, -1)
    gathered = arrived[:, : units_per_dev * unit_width].reshape(all_rows, units_per_dev, unit_width)
    basis_recv = arrived[:, units_per_dev * unit_width :].reshape(all_rows, 2, half_deg)

    band = lax.axis_index("lat")
    unit_ids = units_per_dev * band + jnp.arange(units_per_dev)
    local_wave = unit_ids // 4
    use_last = (local_wave - (units_per_dev * band) // 4) > 0
    basis = jnp.where(
        use_last[None, :, None], basis_recv[:, 1:2, :], basis_recv[:, 0:1, :]
    )
    wavenum = lax.axis_index("lon") * wave_dev + local_wave
    degree = 2 * jnp.arange(half_deg)
    parity = wavenum % 2
    mask_even = degree[None, :] + parity[:, None] >= wavenum[:, None]
    mask_odd = degree[None, :] + 1 - parity[:, None] >= wavenum[:, None]
    north_basis = jnp.where(mask_even[None], basis[:half_rows], jnp.zeros_like(basis[:half_rows]))
    south_basis = jnp.where(mask_odd[None], basis[half_rows:], jnp.zeros_like(basis[half_rows:]))

    north_wide = gathered[:half_rows].astype(jnp.float32)
    south_wide = gathered[half_rows:].astype(jnp.float32)
    comb_even = (north_wide + south_wide).astype(jnp.bfloat16)
    comb_odd = (north_wide - south_wide).astype(jnp.bfloat16)
    deg_even = jnp.einsum(
        "nuk,nuc->ukc", north_basis, comb_even, preferred_element_type=jnp.float32
    ).astype(jnp.bfloat16)
    deg_odd = jnp.einsum(
        "nuk,nuc->ukc", south_basis, comb_odd, preferred_element_type=jnp.float32
    ).astype(jnp.bfloat16)
    proj_even = jnp.einsum(
        "nuk,ukc->nuc", north_basis, deg_even, preferred_element_type=jnp.float32
    ).astype(jnp.bfloat16).astype(jnp.float32)
    proj_odd = jnp.einsum(
        "nuk,ukc->nuc", south_basis, deg_odd, preferred_element_type=jnp.float32
    ).astype(jnp.bfloat16).astype(jnp.float32)
    grad_units = jnp.concatenate([proj_even + proj_odd, proj_even - proj_odd], 0).astype(
        jnp.bfloat16
    )
    returned = lax.all_to_all(
        grad_units.reshape(lat_count, lat_rows, units_per_dev * unit_width), "lat", 0, 0, tiled=True
    ).transpose(1, 0, 2).reshape(lat_rows, 2 * wave_dev, width)

    by_pair = returned.reshape(lon_count // 4, 1, 2, pair_rows, 2 * wave_dev, width)
    pair_send = jnp.broadcast_to(
        by_pair, (lon_count // 4, halves, 2, pair_rows, 2 * wave_dev, width)
    ).reshape(lon_count, pair_rows, 2 * wave_dev, width)
    pair_coeffs = lax.all_to_all(pair_send, "lon", 0, 0, tiled=True)
    half_grid = table_dot(
        table.reshape(group * lon_dev, lon_count, 2 * wave_dev), pair_coeffs, (((1, 2), (0, 2)), ((), ()))
    )
    half_send = half_grid.astype(jnp.bfloat16).reshape(group, lon_dev, pair_rows, width).transpose(0, 2, 1, 3)
    half_send = half_send.reshape(group, pair_rows * lon_dev, width)
    spatial = lax.all_to_all(
        half_send, "lon", 0, 0, tiled=True, axis_index_groups=half_groups
    ).reshape(lat_rows, lon_dev, width)
    mixed = jnp.einsum("rlc,dc->rld", spatial, spectral_weight, preferred_element_type=jnp.float32)
    return (mixed + skip_term).astype(jnp.bfloat16)


def solution(mesh):
    return jax.shard_map(
        shards,
        mesh=mesh,
        in_specs=(P("lat", "lon", None), P("lat", "lon", None), P(), P()),
        out_specs=P("lat", "lon", None),
        check_vma=False,
    )
```
